32 devices in a mesh: grp: 4 (over x, core), rel: 8 (over z, y).
Axes of the slice: x: 2, y: 2, z: 4, core: 2. Of those that a mesh axis runs over, the one named last changes fastest.
Arguments:
- head_ids: int32 [65536], P(('grp', 'rel')), may hold values from 0 to 1023
- relations: int32 [65536, 1], P(('grp', 'rel')), may hold values from 0 to 31; in each aligned block of 2048 rows (0 to 2047, 2048 to 4095, ...) at most 128 rows name the same one
- tail_ids: int32 [65536], P(('grp', 'rel')), may hold values from 0 to 1023
- neg_owner: int32 [1], replicated, may hold values from 0 to 31
- entities: bfloat16 [32768, 512], P(('grp', 'rel')), may hold values from -0.3984375 to 0.3984375
- rel_weight: float32 [32, 512, 512], P('rel'), may hold values from -6 to 6
- rel_accum: float32 [32, 512], P('rel'), may hold values from 0.001 to 0.1
Outputs:
- losses: bfloat16 [65536], P(('grp', 'rel'))
- head_grad: bfloat16 [65536, 512], P(('grp', 'rel'))
- new_rel: float32 [32, 512, 512], P('rel')
- new_accum: float32 [32, 512], P('rel')
The draws below stay inside these ranges and needn't reach their ends.
Inputs may be any that keep to these rules, and one draw needn't show every extreme that they name: `head_ids`: a row of the device's own shard of 1024 entity rows. `tail_ids`: a row of the device's own shard of 1024 entity rows. `relations`: in the 2048 rows of one device no relation is named by more than 128 rows; some relation is named by exactly 128. `neg_owner`: a device index, counted grp first, then rel.
All inputs are finite; a program needn't handle non-finite values.
Results may differ from the reference program's by a relative error of at most 0.0095.
Values may be sent and summed in bfloat16 or wider, within the bound.
No kernel may reach another device: no remote copies, remote signals or barrier semaphores. Data moves between devices by JAX's collectives and lax.ppermute only.
A program may use at most 128 MiB of HBM per device.

```python
import math
import jax
import jax.numpy as jnp
import numpy as np
from jax import lax

D = 512
NEG = 1024
TRIP_DEV = 2048
GROUPS = 4
OWNERS = 8
RELS = 32
CAPR = 128
TRIPLES = 65536
ENTS = 32768
DEVICES = 32


def with_ends(result, stream_key, least, high):
    extent = result.shape
    place = [jax.random.randint(jax.random.fold_in(stream_key, axis), (), 0, extent[axis]) for axis in range(len(extent))]
    result = result.at[tuple(place)].set(least)
    longest = extent.index(max(extent))
    place[longest] = (place[longest] + 1) % extent[longest]
    return result.at[tuple(place)].set(high)


def level_of(key, dims, shards, smallest, high):
    factor_of, own = 1.0, jax.random.fold_in(key, 6)
    for axis_at, shards_of in shards:
        draws = jnp.exp(jax.random.uniform(jax.random.fold_in(own, axis_at), (shards_of,), jnp.float32, smallest / len(shards), high / len(shards)))
        factor_of = factor_of * jnp.repeat(draws, dims[axis_at] // shards_of).reshape([-1 if axis == axis_at else 1 for axis in range(len(dims))])
    return factor_of


def assign_block(key, own, number, rows, number_of, top, limit, slope):
    order = jax.random.permutation(key, number_of)
    crowded, usual = portions_of(number_of, rows * top, limit, slope, True), portions_of(number_of, rows * top, limit, slope, False)
    places = jnp.arange(number_of)

    def named(lengths, offset_by):
        used = int((lengths > 0).sum())
        fixed = max(1, used // 4)
        shifted = fixed + (places - fixed + offset_by * (used - fixed)) % max(1, number_of - fixed)
        return jnp.zeros((number_of,), jnp.int32).at[order[jnp.where(places < fixed, places, shifted)]].set(jnp.asarray(lengths, jnp.int32))

    lengths = jnp.where(number % 4 == 0, named(crowded, number // 4), named(usual, number - number // 4 - 1))
    mixed = jax.random.permutation(jax.random.fold_in(own, 3), number_of)
    donor, taker = mixed[0:number_of // 2 * 2:2], mixed[1:number_of // 2 * 2:2]
    margin = jnp.minimum(lengths[donor] - 1, limit - lengths[taker]) // 2
    margin = jnp.where((donor == order[0]) | (taker == order[0]) | (lengths[taker] == 0), 0, jnp.maximum(margin, 0))
    shifted = jax.random.randint(jax.random.fold_in(own, 4), (number_of // 2,), 0, 1 << 20) % (margin + 1)
    lengths = lengths.at[donor].add(-shifted).at[taker].add(shifted)
    labels = jnp.searchsorted(jnp.cumsum(lengths), jnp.arange(rows * top), side="right").astype(jnp.int32)
    table = labels.reshape(top, rows).T
    table = table[jax.random.permutation(jax.random.fold_in(own, 1), rows)]
    offset_by = jax.random.randint(jax.random.fold_in(own, 2), (rows, 1), 0, top)
    return jnp.take_along_axis(table, (jnp.arange(top)[None, :] + offset_by) % top, axis=1)


def portions_of(count, total, most, skew, full):
    portions = [(1 << 20) // math.isqrt(grade ** skew) + 1 for grade in range(1, count + 1)]
    largest = most if full else min(most, max(-(-total // count), total * portions[0] // sum(portions)))
    least = 1 if total - largest >= count - 1 else 0
    counts, rest = [largest] + [least] * (count - 1), total - largest - least * (count - 1)
    while rest > 0:
        free = [i for i in range(1, count) if counts[i] < largest] or [i for i in range(1, count) if counts[i] < most]
        mass, remaining = sum([portions[i] for i in free]), rest
        for i in free:
            addition = min(most - counts[i], max(1, remaining * portions[i] // mass), rest)
            counts[i] = counts[i] + addition
            rest = rest - addition
    return np.array(counts)


def noise(stream_key, extent, deviation, bound, split=(), held_as=jnp.bfloat16):
    entries = jax.random.normal(stream_key, extent, jnp.float32) * deviation
    if len(split) > 0:
        entries = level_of(stream_key, extent, split, -0.22, 0.18) * entries
    return jnp.clip(entries, min=-bound, max=bound).astype(held_as)


def setup_inputs(seed: int = 0) -> dict:
    key_list = jax.random.split(jax.random.key(seed), 8)
    head_ids = with_ends(jax.random.randint(key_list[0], (TRIPLES,), 0, NEG), jax.random.fold_in(key_list[0], 1), 0, NEG - 1).astype(jnp.int32)
    relations_keys = jax.random.split(jax.random.fold_in(key_list[1], 1), TRIPLES // TRIP_DEV)
    relations_turns = jax.random.permutation(jax.random.fold_in(key_list[1], 3), TRIPLES // TRIP_DEV)
    relations = jax.vmap(lambda own, number: assign_block(jax.random.fold_in(key_list[1], 2), own, number, TRIP_DEV, RELS, 1, CAPR, 2))(relations_keys, relations_turns).reshape((TRIPLES, 1))
    tail_ids = with_ends(jax.random.randint(key_list[2], (TRIPLES,), 0, NEG), jax.random.fold_in(key_list[2], 1), 0, NEG - 1).astype(jnp.int32)
    neg_owner = jax.random.randint(key_list[3], (1,), 0, DEVICES).astype(jnp.int32)
    entities = noise(key_list[4], (ENTS, D), 0.1, 0.3984375, ((0, 32),))
    rel_weight = noise(key_list[5], (RELS, D, D), 1.0, 6.0, ((0, 8),), jnp.float32)
    rel_accum = jnp.clip(jnp.exp(math.log(0.1) - 4.6051702 * jax.random.uniform(key_list[6], (RELS, D), jnp.float32) ** level_of(key_list[6], (RELS, D), ((0, 8),), -0.2, 0.2)), 0.001, 0.1)
    return dict(head_ids=head_ids, relations=relations, tail_ids=tail_ids, neg_owner=neg_owner, entities=entities, rel_weight=rel_weight, rel_accum=rel_accum)


LEARNING_RATE = 1.0

def slot_ranks(rel_ids, bucket_count):
    one_hot = (rel_ids[..., None] == jnp.arange(bucket_count, dtype=jnp.int32)).astype(jnp.int32)
    running = jnp.cumsum(one_hot, axis=-2) - 1
    return lax.optimization_barrier(jnp.sum(one_hot * running, axis=-1)).astype(jnp.int32)

def score_rows(query_rows, tail_rows, negatives):
    positive = lax.optimization_barrier(jnp.sum(query_rows.astype(jnp.float32) * tail_rows.astype(jnp.float32), axis=-1))
    neg_scores = jnp.dot(query_rows, negatives.T, preferred_element_type=jnp.float32)
    losses = jax.nn.softplus(-positive) + lax.optimization_barrier(jnp.mean(jax.nn.softplus(neg_scores), axis=-1))
    coefs = (jax.nn.sigmoid(neg_scores) / negatives.shape[0]).astype(jnp.bfloat16)
    grad_query = -jax.nn.sigmoid(-positive)[:, None] * tail_rows.astype(jnp.float32)
    grad_query = grad_query + jnp.dot(coefs, negatives, preferred_element_type=jnp.float32)
    return (losses.astype(jnp.bfloat16), grad_query.astype(jnp.bfloat16))

def adagrad(weight, accumulator, gradient):
    new_accum = accumulator + lax.optimization_barrier(jnp.mean(gradient * gradient, axis=-1))
    return (weight - LEARNING_RATE * gradient / jnp.sqrt(new_accum)[..., None], new_accum)

def reference(head_ids, relations, tail_ids, neg_owner, entities, rel_weight, rel_accum):
    width = entities.shape[1]
    rel_ids = relations[:, 0].astype(jnp.int32)
    device = jnp.arange(TRIPLES, dtype=jnp.int32) // TRIP_DEV
    head_rows = jnp.take(entities, device * NEG + head_ids, axis=0)
    tail_rows = jnp.take(entities, device * NEG + tail_ids, axis=0)
    negatives = lax.dynamic_slice_in_dim(entities, (neg_owner[0] * NEG).astype(jnp.int32), NEG, 0)
    ranking = slot_ranks(rel_ids.reshape(DEVICES, TRIP_DEV), RELS).reshape(TRIPLES)
    flat_index = device * (RELS * CAPR) + rel_ids * CAPR + ranking
    matrices = rel_weight.astype(jnp.bfloat16)

    def by_relation(values):
        filled = jnp.zeros((DEVICES * RELS * CAPR, width), values.dtype).at[flat_index].set(values)
        return filled.reshape(DEVICES, RELS, CAPR, width).transpose(1, 0, 2, 3).reshape(RELS, DEVICES * CAPR, width)

    def by_triple(stacked):
        whole = stacked.reshape(RELS, DEVICES, CAPR, width).transpose(1, 0, 2, 3)
        return whole.reshape(DEVICES * RELS * CAPR, width)[flat_index]
    held_rows = by_relation(head_rows)

    def project(operands):
        rows_in, matrix = operands
        return jnp.dot(rows_in, matrix, preferred_element_type=jnp.float32).astype(jnp.bfloat16)
    projected = by_triple(lax.map(project, (held_rows, matrices)))

    def score_block(operands):
        query_block, tail_block = operands
        return score_rows(query_block, tail_block, negatives)
    losses, grad_query = lax.map(score_block, (projected.reshape(DEVICES, TRIP_DEV, width), tail_rows.reshape(DEVICES, TRIP_DEV, width)))
    grad_rows = by_relation(grad_query.reshape(TRIPLES, width))

    def backward(operands):
        rows_in, grad_in, matrix = operands
        head_back = jnp.dot(grad_in, matrix.T, preferred_element_type=jnp.float32).astype(jnp.bfloat16)
        rows_group = rows_in.reshape(GROUPS, OWNERS * CAPR, width).astype(jnp.float32)
        grad_group = grad_in.reshape(GROUPS, OWNERS * CAPR, width).astype(jnp.float32)
        partial_value = jnp.einsum('gnd,gne->gde', rows_group, grad_group).astype(jnp.bfloat16)
        partial_value = lax.optimization_barrier(partial_value)
        return (head_back, lax.optimization_barrier(jnp.sum(partial_value.astype(jnp.float32), axis=0)))
    head_stack, summed = lax.map(backward, (held_rows, grad_rows, matrices))
    head_grad = by_triple(head_stack)
    new_rel, new_accum = adagrad(rel_weight, rel_accum, summed)
    return (losses.reshape(TRIPLES), head_grad, new_rel, new_accum)
```

```python
import jax
import jax.numpy as jnp
from jax import lax
from jax.sharding import PartitionSpec as P

LEARNING_RATE = 1.0
BF = jnp.bfloat16
F32 = jnp.float32


def broadcast(shard, axis, root):
    mine = lax.axis_index(axis) == root
    return lax.psum(jnp.where(mine, shard, jnp.zeros_like(shard)), axis)


def one_hot(ids, count):
    return (ids[:, None] == jnp.arange(count, dtype=jnp.int32)[None, :]).astype(BF)


def select_rows(selector, rows):
    return jnp.dot(selector, rows, preferred_element_type=F32).astype(BF)


def select_back(selector, rows):
    return lax.dot_general(
        selector, rows, (((0,), (0,)), ((), ())), preferred_element_type=F32
    ).astype(BF)


def score_rows(query_rows, tail_rows, negatives):
    positive = jnp.sum(query_rows.astype(F32) * tail_rows.astype(F32), axis=-1)
    neg_scores = lax.dot_general(
        query_rows, negatives, (((1,), (1,)), ((), ())), preferred_element_type=F32
    )
    losses = jax.nn.softplus(-positive) + jnp.mean(jax.nn.softplus(neg_scores), axis=-1)
    coefs = (jax.nn.sigmoid(neg_scores) / negatives.shape[0]).astype(BF)
    grad_query = -jax.nn.sigmoid(-positive)[:, None] * tail_rows.astype(F32)
    grad_query = grad_query + jnp.dot(coefs, negatives, preferred_element_type=F32)
    return (losses.astype(BF), grad_query.astype(BF))


def adagrad(weight, accumulator, gradient):
    new_accum = accumulator + jnp.mean(gradient * gradient, axis=-1)
    return (weight - LEARNING_RATE * gradient / jnp.sqrt(new_accum)[..., None], new_accum)


def broadcast_rows(shard, axis, root):
    mine = lax.axis_index(axis) == root
    return lax.psum(jnp.where(mine, shard, jnp.zeros_like(shard)), axis)


def slot_ranks(rel_ids, bucket_count):
    one_hot = (rel_ids[..., None] == jnp.arange(bucket_count, dtype=jnp.int32)).astype(jnp.int32)
    running = jnp.cumsum(one_hot, axis=-2) - 1
    return jnp.sum(one_hot * running, axis=-1)


def score_rows_rows(query_rows, tail_rows, negatives):
    positive = jnp.sum(query_rows.astype(jnp.float32) * tail_rows.astype(jnp.float32), axis=-1)
    neg_scores = jnp.dot(query_rows, negatives.T, preferred_element_type=jnp.float32)
    losses = jax.nn.softplus(-positive) + jnp.mean(jax.nn.softplus(neg_scores), axis=-1)
    coefs = (jax.nn.sigmoid(neg_scores) / negatives.shape[0]).astype(jnp.bfloat16)
    grad_query = -jax.nn.sigmoid(-positive)[:, None] * tail_rows.astype(jnp.float32)
    grad_query = grad_query + jnp.dot(coefs, negatives, preferred_element_type=jnp.float32)
    return (losses.astype(jnp.bfloat16), grad_query.astype(jnp.bfloat16))


def adagrad_rows(weight, accumulator, gradient):
    new_accum = accumulator + jnp.mean(gradient * gradient, axis=-1)
    return (weight - LEARNING_RATE * gradient / jnp.sqrt(new_accum)[..., None], new_accum)


def to_buckets(values, position, layout):
    flat_shape = (layout[0] * layout[1] * layout[2],) + values.shape[1:]
    filled = jnp.zeros(flat_shape, values.dtype).at[position].set(values)
    return filled.reshape(layout + values.shape[1:])


def from_buckets(stacked, position):
    return stacked.reshape((-1,) + stacked.shape[3:])[position]


def per_device_rows(head_ids, relations, tail_ids, neg_owner, entities, rel_weight, rel_accum):
    rows_here = head_ids.shape[0]
    width = entities.shape[1]
    owner_count = lax.axis_size("rel")
    local_rels = rel_weight.shape[0]
    capacity = 2 * rows_here // (owner_count * local_rels)
    layout = (owner_count, local_rels, capacity)
    rel_ids = relations[:, 0]
    position = rel_ids * capacity + slot_ranks(rel_ids, owner_count * local_rels)
    head_rows = jnp.take(entities, head_ids, axis=0)
    tail_rows = jnp.take(entities, tail_ids, axis=0)
    matrices = rel_weight.astype(jnp.bfloat16)
    negatives = broadcast_rows(entities, ("grp", "rel"), neg_owner[0])
    held_rows, held_tails = (
        lax.all_to_all(
            to_buckets(head_rows, position, layout), "rel", split_axis=0, concat_axis=0, tiled=True
        ),
        lax.all_to_all(
            to_buckets(tail_rows, position, layout), "rel", split_axis=0, concat_axis=0, tiled=True
        ),
    )
    projected = jnp.einsum(
        "srcd,rde->srce", held_rows, matrices, preferred_element_type=jnp.float32
    ).astype(jnp.bfloat16)
    slot_losses, slot_grads = score_rows_rows(
        projected.reshape(-1, width), held_tails.reshape(-1, width), negatives
    )
    grad_rows = slot_grads.reshape(held_rows.shape)
    partial_value = jnp.einsum(
        "srcd,srce->rde", held_rows, grad_rows, preferred_element_type=jnp.float32
    )
    head_back = jnp.einsum(
        "srce,rde->srcd", grad_rows, matrices, preferred_element_type=jnp.float32
    ).astype(jnp.bfloat16)
    partial_value, head_back = (partial_value, head_back)
    back_grads, back_losses = (
        lax.all_to_all(head_back, "rel", split_axis=0, concat_axis=0, tiled=True),
        lax.all_to_all(slot_losses.reshape(layout), "rel", split_axis=0, concat_axis=0, tiled=True),
    )
    head_grad = from_buckets(back_grads, position)
    losses = from_buckets(back_losses, position)
    summed = lax.psum(partial_value.astype(jnp.bfloat16), "grp").astype(jnp.float32)
    new_rel, new_accum = adagrad_rows(rel_weight, rel_accum, summed)
    return (losses, head_grad, new_rel, new_accum)


def per_device(head_ids, relations, tail_ids, neg_owner, entities, rel_weight, rel_accum):
    rows_here = head_ids.shape[0]
    width = entities.shape[1]
    shard_rows = entities.shape[0]
    owner_count = lax.axis_size("rel")
    local_rels = rel_weight.shape[0]
    rel_count = owner_count * local_rels
    capacity = 2 * rows_here // rel_count
    slots = rel_count * capacity

    half = local_rels // 2
    core = lax.axis_index("core")
    mine = lax.dynamic_slice_in_dim(rel_weight, core * half, half, 0).astype(BF)
    matrices = lax.all_gather(mine, "rel", axis=0, tiled=False)
    matrices = lax.all_gather(matrices, "core", axis=1, tiled=False)
    matrices = matrices.reshape(rel_count, width, width)
    negatives = broadcast(entities, ("x", "core", "rel"), neg_owner[0])

    rel_ids = relations[:, 0]
    rel_hot = one_hot(rel_ids, rel_count)
    order = jnp.arange(rows_here, dtype=jnp.int32)
    lower = (order[:, None] >= order[None, :]).astype(BF)
    running = jnp.dot(lower, rel_hot, preferred_element_type=F32)
    rank = jnp.sum(running * rel_hot.astype(F32), axis=-1).astype(jnp.int32) - 1
    position = rel_ids * capacity + rank
    bucket = (jnp.arange(slots, dtype=jnp.int32)[:, None] == position[None, :]).astype(BF)

    head_rows = select_rows(one_hot(head_ids, shard_rows), entities)
    tail_rows = select_rows(one_hot(tail_ids, shard_rows), entities)
    held_rows = select_rows(bucket, head_rows).reshape(rel_count, capacity, width)

    projected = jnp.einsum(
        "rcd,rde->rce", held_rows, matrices, preferred_element_type=F32
    ).astype(BF)
    query_rows = select_back(bucket, projected.reshape(slots, width))
    losses, grad_query = score_rows(query_rows, tail_rows, negatives)
    grad_rows = select_rows(bucket, grad_query).reshape(rel_count, capacity, width)

    partial_value = jnp.einsum(
        "rcd,rce->rde", held_rows, grad_rows, preferred_element_type=F32
    ).astype(BF)
    partial_value = partial_value.reshape(owner_count, 2, half, width, width)
    summed = lax.psum_scatter(partial_value, "core", scatter_dimension=1, tiled=True)
    summed = lax.psum_scatter(summed, "rel", scatter_dimension=0, tiled=True)
    summed = lax.psum(summed.reshape(half, width, width), "x")
    summed = lax.all_gather(summed, "core", axis=0, tiled=True).astype(F32)

    head_back = jnp.einsum(
        "rce,rde->rcd", grad_rows, matrices, preferred_element_type=F32
    ).astype(BF)
    head_grad = select_back(bucket, head_back.reshape(slots, width))

    new_rel, new_accum = adagrad(rel_weight, rel_accum, summed)
    return (losses, head_grad, new_rel, new_accum)


GATHER_LIMIT = 16 * 1024 * 1024


def solution(mesh):
    placed = (
        P(("grp", "rel")),
        P(("grp", "rel"), None),
        P(("grp", "rel")),
        P(),
        P(("grp", "rel"), None),
        P("rel", None, None),
        P("rel", None),
    )
    outs = (
        P(("grp", "rel")),
        P(("grp", "rel"), None),
        P("rel", None, None),
        P("rel", None),
    )
    rows_step = jax.shard_map(
        per_device_rows, mesh=mesh, in_specs=placed, out_specs=outs, check_vma=False
    )
    groups, owners = mesh.devices.shape
    split = jax.sharding.Mesh(mesh.devices.reshape(groups // 2, 2, owners), ("x", "core", "rel"))

    def respec(spec):
        return P(*[("x", "core", "rel") if part == ("grp", "rel") else part for part in spec])

    local_step = jax.shard_map(
        per_device,
        mesh=split,
        in_specs=tuple(respec(s) for s in placed),
        out_specs=tuple(respec(s) for s in outs),
        check_vma=False,
    )

    def step(head_ids, relations, tail_ids, neg_owner, entities, rel_weight, rel_accum):
        args = (head_ids, relations, tail_ids, neg_owner, entities, rel_weight, rel_accum)
        width = rel_weight.shape[-1]
        if rel_weight.shape[0] * width * width * 2 <= GATHER_LIMIT:
            return local_step(*args)
        return rows_step(*args)

    return step
```

```python
import jax
import jax.numpy as jnp
from jax import lax
from jax.sharding import PartitionSpec as P

LEARNING_RATE = 1.0


def broadcast(shard, axis, root):
    mine = lax.axis_index(axis) == root
    return lax.psum(jnp.where(mine, shard, jnp.zeros_like(shard)), axis)


def score_rows(query_rows, tail_rows, negatives):
    positive = jnp.sum(query_rows.astype(jnp.float32) * tail_rows.astype(jnp.float32), axis=-1)
    neg_scores = jnp.dot(query_rows, negatives.T, preferred_element_type=jnp.float32)
    losses = jax.nn.softplus(-positive) + jnp.mean(jax.nn.softplus(neg_scores), axis=-1)
    coefs = (jax.nn.sigmoid(neg_scores) / negatives.shape[0]).astype(jnp.bfloat16)
    grad_query = -jax.nn.sigmoid(-positive)[:, None] * tail_rows.astype(jnp.float32)
    grad_query = grad_query + jnp.dot(coefs, negatives, preferred_element_type=jnp.float32)
    return (losses.astype(jnp.bfloat16), grad_query.astype(jnp.bfloat16))


def adagrad(weight, accumulator, gradient):
    new_accum = accumulator + jnp.mean(gradient * gradient, axis=-1)
    return (weight - LEARNING_RATE * gradient / jnp.sqrt(new_accum)[..., None], new_accum)


def one_hot(ids, count):
    return (ids[:, None] == jnp.arange(count, dtype=jnp.int32)[None, :]).astype(jnp.bfloat16)


def select_rows(selector, rows):
    return jnp.dot(selector, rows, preferred_element_type=jnp.float32).astype(jnp.bfloat16)


def per_device(head_ids, relations, tail_ids, neg_owner, entities, rel_weight, rel_accum):
    rows_here = head_ids.shape[0]
    width = entities.shape[1]
    shard_rows = entities.shape[0]
    owner_count = lax.axis_size("rel")
    local_rels = rel_weight.shape[0]
    rel_count = owner_count * local_rels
    capacity = 2 * rows_here // rel_count
    layout = (owner_count, local_rels, capacity)
    slots = rel_count * capacity
    negatives = broadcast(entities, ("grp", "rel"), neg_owner[0])
    rel_ids = relations[:, 0]
    rel_hot = one_hot(rel_ids, rel_count)
    order = jnp.arange(rows_here, dtype=jnp.int32)
    lower = (order[:, None] >= order[None, :]).astype(jnp.bfloat16)
    running = jnp.dot(lower, rel_hot, preferred_element_type=jnp.float32)
    rank = jnp.sum(running * rel_hot.astype(jnp.float32), axis=-1).astype(jnp.int32) - 1
    position = rel_ids * capacity + rank
    ids = jnp.stack([head_ids, tail_ids], axis=-1) + 1
    slot_ids = jnp.zeros((slots, 2), jnp.int32).at[position].set(ids) - 1
    held_rows = select_rows(one_hot(slot_ids[:, 0], shard_rows), entities).reshape(layout + (width,))
    held_rows = lax.all_to_all(held_rows, "rel", split_axis=0, concat_axis=0, tiled=True)
    tail_send = select_rows(one_hot(slot_ids[:, 1], shard_rows), entities).reshape(layout + (width,))
    held_tails = lax.all_to_all(tail_send, "rel", split_axis=0, concat_axis=0, tiled=True)
    matrices = rel_weight.astype(jnp.bfloat16)
    projected = jnp.einsum(
        "srcd,rde->srce", held_rows, matrices, preferred_element_type=jnp.float32
    ).astype(jnp.bfloat16)
    slot_losses, slot_grads = score_rows(
        projected.reshape(-1, width), held_tails.reshape(-1, width), negatives
    )
    grad_rows = slot_grads.reshape(held_rows.shape)
    partial_value = jnp.einsum(
        "srcd,srce->rde", held_rows, grad_rows, preferred_element_type=jnp.float32
    )
    summed = lax.psum(partial_value.astype(jnp.bfloat16), "grp").astype(jnp.float32)
    head_back = jnp.einsum(
        "srce,rde->srcd", grad_rows, matrices, preferred_element_type=jnp.float32
    ).astype(jnp.bfloat16)
    per_owner = local_rels * capacity
    extra = -(-per_owner // width)
    loss_rows = slot_losses.reshape(owner_count, per_owner)
    loss_rows = jnp.pad(loss_rows, ((0, 0), (0, extra * width - per_owner)))
    loss_rows = loss_rows.reshape(owner_count, extra, width)
    packed = jnp.concatenate([head_back.reshape(owner_count, per_owner, width), loss_rows], axis=1)
    packed = lax.all_to_all(packed, "rel", split_axis=0, concat_axis=0, tiled=True)
    back_grads = packed[:, :per_owner].reshape(slots, width)
    back_losses = packed[:, per_owner:].reshape(owner_count, extra * width)
    back_losses = back_losses[:, :per_owner].reshape(slots)
    taken = one_hot(position, slots)
    head_grad = select_rows(taken, back_grads)
    losses = jnp.dot(taken, back_losses, preferred_element_type=jnp.float32).astype(jnp.bfloat16)
    new_rel, new_accum = adagrad(rel_weight, rel_accum, summed)
    return (losses, head_grad, new_rel, new_accum)


def solution(mesh):
    placed = (
        P(("grp", "rel")),
        P(("grp", "rel"), None),
        P(("grp", "rel")),
        P(),
        P(("grp", "rel"), None),
        P("rel", None, None),
        P("rel", None),
    )
    return jax.shard_map(
        per_device,
        mesh=mesh,
        in_specs=placed,
        out_specs=(
            P(("grp", "rel")),
            P(("grp", "rel"), None),
            P("rel", None, None),
            P("rel", None),
        ),
        check_vma=False,
    )
```

```python
import jax
import jax.numpy as jnp
from jax import lax
from jax.sharding import PartitionSpec as P

LEARNING_RATE = 1.0
CHUNKS = 2


def broadcast(shard, axis, root):
    mine = lax.axis_index(axis) == root
    return lax.psum(jnp.where(mine, shard, jnp.zeros_like(shard)), axis)


def score_rows(query_rows, tail_rows, negatives):
    positive = jnp.sum(query_rows.astype(jnp.float32) * tail_rows.astype(jnp.float32), axis=-1)
    neg_scores = jnp.dot(query_rows, negatives.T, preferred_element_type=jnp.float32)
    losses = jax.nn.softplus(-positive) + jnp.mean(jax.nn.softplus(neg_scores), axis=-1)
    coefs = (jax.nn.sigmoid(neg_scores) / negatives.shape[0]).astype(jnp.bfloat16)
    grad_query = -jax.nn.sigmoid(-positive)[:, None] * tail_rows.astype(jnp.float32)
    grad_query = grad_query + jnp.dot(coefs, negatives, preferred_element_type=jnp.float32)
    return (losses.astype(jnp.bfloat16), grad_query.astype(jnp.bfloat16))


def adagrad(weight, accumulator, gradient):
    new_accum = accumulator + jnp.mean(gradient * gradient, axis=-1)
    return (weight - LEARNING_RATE * gradient / jnp.sqrt(new_accum)[..., None], new_accum)


def one_hot(ids, count):
    return (ids[:, None] == jnp.arange(count, dtype=jnp.int32)[None, :]).astype(jnp.bfloat16)


def select_rows(selector, rows):
    return jnp.dot(selector, rows, preferred_element_type=jnp.float32).astype(jnp.bfloat16)


def per_device(head_ids, relations, tail_ids, neg_owner, entities, rel_weight, rel_accum):
    rows_here = head_ids.shape[0]
    width = entities.shape[1]
    shard_rows = entities.shape[0]
    owner_count = lax.axis_size("rel")
    local_rels = rel_weight.shape[0]
    rel_count = owner_count * local_rels
    capacity = 2 * rows_here // rel_count
    layout = (owner_count, local_rels, capacity)
    slots = rel_count * capacity
    negatives = broadcast(entities, ("grp", "rel"), neg_owner[0])
    rel_ids = relations[:, 0]
    rel_hot = one_hot(rel_ids, rel_count)
    order = jnp.arange(rows_here, dtype=jnp.int32)
    lower = (order[:, None] >= order[None, :]).astype(jnp.bfloat16)
    running = jnp.dot(lower, rel_hot, preferred_element_type=jnp.float32)
    rank = jnp.sum(running * rel_hot.astype(jnp.float32), axis=-1).astype(jnp.int32) - 1
    position = rel_ids * capacity + rank
    ids = jnp.stack([head_ids, tail_ids], axis=-1) + 1
    slot_ids = jnp.zeros((slots, 2), jnp.int32).at[position].set(ids) - 1
    held_all = select_rows(one_hot(slot_ids[:, 0], shard_rows), entities).reshape(layout + (width,))
    tail_all = select_rows(one_hot(slot_ids[:, 1], shard_rows), entities).reshape(layout + (width,))
    matrices = rel_weight.astype(jnp.bfloat16)
    part = local_rels // CHUNKS
    per_owner = part * capacity
    extra = -(-per_owner // width)
    partials, backs, back_loss = [], [], []
    for chunk in range(CHUNKS):
        pick = slice(chunk * part, (chunk + 1) * part)
        held_rows = lax.all_to_all(held_all[:, pick], "rel", split_axis=0, concat_axis=0, tiled=True)
        held_tails = lax.all_to_all(tail_all[:, pick], "rel", split_axis=0, concat_axis=0, tiled=True)
        weights = matrices[pick]
        projected = jnp.einsum(
            "srcd,rde->srce", held_rows, weights, preferred_element_type=jnp.float32
        ).astype(jnp.bfloat16)
        slot_losses, slot_grads = score_rows(
            projected.reshape(-1, width), held_tails.reshape(-1, width), negatives
        )
        grad_rows = slot_grads.reshape(held_rows.shape)
        partials.append(jnp.einsum(
            "srcd,srce->rde", held_rows, grad_rows, preferred_element_type=jnp.float32
        ))
        head_back = jnp.einsum(
            "srce,rde->srcd", grad_rows, weights, preferred_element_type=jnp.float32
        ).astype(jnp.bfloat16)
        loss_rows = slot_losses.reshape(owner_count, per_owner)
        loss_rows = jnp.pad(loss_rows, ((0, 0), (0, extra * width - per_owner)))
        loss_rows = loss_rows.reshape(owner_count, extra, width)
        packed = jnp.concatenate([head_back.reshape(owner_count, per_owner, width), loss_rows], axis=1)
        packed = lax.all_to_all(packed, "rel", split_axis=0, concat_axis=0, tiled=True)
        backs.append(packed[:, :per_owner].reshape(owner_count, part, capacity, width))
        loss_back = packed[:, per_owner:].reshape(owner_count, extra * width)[:, :per_owner]
        back_loss.append(loss_back.reshape(owner_count, part, capacity))
    partial_value = jnp.concatenate(partials, axis=0)
    summed = lax.psum(partial_value.astype(jnp.bfloat16), "grp").astype(jnp.float32)
    back_grads = jnp.concatenate(backs, axis=1).reshape(slots, width)
    back_losses = jnp.concatenate(back_loss, axis=1).reshape(slots)
    taken = one_hot(position, slots)
    head_grad = select_rows(taken, back_grads)
    losses = jnp.dot(taken, back_losses, preferred_element_type=jnp.float32).astype(jnp.bfloat16)
    new_rel, new_accum = adagrad(rel_weight, rel_accum, summed)
    return (losses, head_grad, new_rel, new_accum)


def solution(mesh):
    placed = (
        P(("grp", "rel")),
        P(("grp", "rel"), None),
        P(("grp", "rel")),
        P(),
        P(("grp", "rel"), None),
        P("rel", None, None),
        P("rel", None),
    )
    return jax.shard_map(
        per_device,
        mesh=mesh,
        in_specs=placed,
        out_specs=(
            P(("grp", "rel")),
            P(("grp", "rel"), None),
            P("rel", None, None),
            P("rel", None),
        ),
        check_vma=False,
    )
```

```python
import jax
import jax.numpy as jnp
from jax import lax
from jax.sharding import PartitionSpec as P

LEARNING_RATE = 1.0


def broadcast(shard, axis, root):
    mine = lax.axis_index(axis) == root
    return lax.psum(jnp.where(mine, shard, jnp.zeros_like(shard)), axis)


def score_rows(query_rows, tail_rows, negatives):
    positive = jnp.sum(query_rows.astype(jnp.float32) * tail_rows.astype(jnp.float32), axis=-1)
    neg_scores = jnp.dot(query_rows, negatives.T, preferred_element_type=jnp.float32)
    losses = jax.nn.softplus(-positive) + jnp.mean(jax.nn.softplus(neg_scores), axis=-1)
    coefs = (jax.nn.sigmoid(neg_scores) / negatives.shape[0]).astype(jnp.bfloat16)
    grad_query = -jax.nn.sigmoid(-positive)[:, None] * tail_rows.astype(jnp.float32)
    grad_query = grad_query + jnp.dot(coefs, negatives, preferred_element_type=jnp.float32)
    return (losses.astype(jnp.bfloat16), grad_query.astype(jnp.bfloat16))


def adagrad(weight, accumulator, gradient):
    new_accum = accumulator + jnp.mean(gradient * gradient, axis=-1)
    return (weight - LEARNING_RATE * gradient / jnp.sqrt(new_accum)[..., None], new_accum)


def one_hot(ids, count):
    return (ids[:, None] == jnp.arange(count, dtype=jnp.int32)[None, :]).astype(jnp.bfloat16)


def select_rows(selector, rows):
    return jnp.dot(selector, rows, preferred_element_type=jnp.float32).astype(jnp.bfloat16)


def per_device(head_ids, relations, tail_ids, neg_owner, entities, rel_weight, rel_accum):
    rows_here = head_ids.shape[0]
    width = entities.shape[1]
    shard_rows = entities.shape[0]
    owner_count = lax.axis_size("rel")
    local_rels = rel_weight.shape[0]
    rel_count = owner_count * local_rels
    capacity = 2 * rows_here // rel_count
    layout = (owner_count, local_rels, capacity)
    slots = rel_count * capacity
    negatives = broadcast(entities, ("grp", "rel"), neg_owner[0])
    rel_ids = relations[:, 0]
    rel_hot = one_hot(rel_ids, rel_count)
    order = jnp.arange(rows_here, dtype=jnp.int32)
    lower = (order[:, None] >= order[None, :]).astype(jnp.bfloat16)
    running = jnp.dot(lower, rel_hot, preferred_element_type=jnp.float32)
    rank = jnp.sum(running * rel_hot.astype(jnp.float32), axis=-1).astype(jnp.int32) - 1
    position = rel_ids * capacity + rank
    ids = jnp.stack([head_ids, tail_ids], axis=-1) + 1
    slot_ids = jnp.zeros((slots, 2), jnp.int32).at[position].set(ids) - 1
    held_rows = select_rows(one_hot(slot_ids[:, 0], shard_rows), entities).reshape(layout + (width,))
    held_rows = lax.all_to_all(held_rows, "rel", split_axis=0, concat_axis=0, tiled=True)
    tail_send = select_rows(one_hot(slot_ids[:, 1], shard_rows), entities).reshape(layout + (width,))
    held_tails = lax.all_to_all(tail_send, "rel", split_axis=0, concat_axis=0, tiled=True)
    matrices = rel_weight.astype(jnp.bfloat16)
    projected = jnp.einsum(
        "srcd,rde->srce", held_rows, matrices, preferred_element_type=jnp.float32
    ).astype(jnp.bfloat16)
    slot_losses, slot_grads = score_rows(
        projected.reshape(-1, width), held_tails.reshape(-1, width), negatives
    )
    grad_rows = slot_grads.reshape(held_rows.shape)
    partial_value = jnp.einsum(
        "srcd,srce->rde", held_rows, grad_rows, preferred_element_type=jnp.float32
    )
    summed = lax.psum(partial_value.astype(jnp.bfloat16), "grp").astype(jnp.float32)
    head_back = jnp.einsum(
        "srce,rde->srcd", grad_rows, matrices, preferred_element_type=jnp.float32
    ).astype(jnp.bfloat16)
    per_owner = local_rels * capacity
    extra = -(-per_owner // width)
    loss_rows = slot_losses.reshape(owner_count, per_owner)
    loss_rows = jnp.pad(loss_rows, ((0, 0), (0, extra * width - per_owner)))
    loss_rows = loss_rows.reshape(owner_count, extra, width)
    packed = jnp.concatenate([head_back.reshape(owner_count, per_owner, width), loss_rows], axis=1)
    packed = lax.all_to_all(packed, "rel", split_axis=0, concat_axis=0, tiled=True)
    back_grads = packed[:, :per_owner].reshape(slots, width)
    back_losses = packed[:, per_owner:].reshape(owner_count, extra * width)
    back_losses = back_losses[:, :per_owner].reshape(slots)
    taken = one_hot(position, slots)
    head_grad = select_rows(taken, back_grads)
    losses = jnp.dot(taken, back_losses, preferred_element_type=jnp.float32).astype(jnp.bfloat16)
    new_rel, new_accum = adagrad(rel_weight, rel_accum, summed)
    return (losses, head_grad, new_rel, new_accum)


RING = (0, 2, 4, 6, 7, 5, 3, 1)


def ring_tables():
    where = [0] * len(RING)
    for spot, rel in enumerate(RING):
        where[rel] = spot
    return jnp.array(RING, jnp.int32), jnp.array(where, jnp.int32)


def ring_pairs(step):
    count = len(RING)
    return [(RING[p], RING[(p + step) % count]) for p in range(count)]


def ring_collect(piece, step):
    count = len(RING)
    order, where = ring_tables()
    me = lax.axis_index("rel")
    spot = where[me]
    out = jnp.zeros((count,) + piece.shape, piece.dtype)
    out = lax.dynamic_update_index_in_dim(out, piece, me, 0)
    current = piece
    for hop in range(1, count):
        current = lax.ppermute(current, "rel", ring_pairs(step))
        source = order[(spot - step * hop) % count]
        out = lax.dynamic_update_index_in_dim(out, current, source, 0)
    return out


def ring_reduce(blocks, step):
    count = len(RING)
    order, where = ring_tables()
    spot = where[lax.axis_index("rel")]

    def own(offset):
        return lax.dynamic_index_in_dim(blocks, order[(spot - step * offset) % count], 0, False)

    acc = own(1)
    for hop in range(1, count):
        received = lax.ppermute(acc, "rel", ring_pairs(step))
        total = received.astype(jnp.float32) + own(hop + 1).astype(jnp.float32)
        acc = total if hop == count - 1 else total.astype(jnp.bfloat16)
    return acc


def swap(value, axis):
    return lax.ppermute(value, axis, [(0, 1), (1, 0)])


def per_device_local(head_ids, relations, tail_ids, neg_owner, entities, rel_weight, rel_accum):
    rows_here = head_ids.shape[0]
    width = entities.shape[1]
    shard_rows = entities.shape[0]
    owner_count = lax.axis_size("rel")
    local_rels = rel_weight.shape[0]
    half = local_rels // 2
    rel_count = owner_count * local_rels
    capacity = 2 * rows_here // rel_count
    slots = rel_count * capacity
    core = lax.axis_index("core")

    mine = lax.dynamic_slice_in_dim(rel_weight, core * half, half, 0).astype(jnp.bfloat16)
    mine = mine.reshape(2, half // 2, width, width)
    gathered = jnp.concatenate([ring_collect(mine[0], 1), ring_collect(mine[1], -1)], axis=1)
    partner = swap(gathered, "core")
    matrices = jnp.stack([gathered, partner], axis=1).reshape(rel_count, width, width)
    negatives = broadcast(entities, ("x", "core", "rel"), neg_owner[0])

    rel_ids = relations[:, 0]
    spot = rel_ids % local_rels
    side = (spot // half + core) % 2
    slot_rel = (rel_ids // local_rels) * local_rels + side * half + spot % half
    rel_hot = one_hot(slot_rel, rel_count)
    order = jnp.arange(rows_here, dtype=jnp.int32)
    lower = (order[:, None] >= order[None, :]).astype(jnp.bfloat16)
    running = jnp.dot(lower, rel_hot, preferred_element_type=jnp.float32)
    rank = jnp.sum(running * rel_hot.astype(jnp.float32), axis=-1).astype(jnp.int32) - 1
    position = slot_rel * capacity + rank
    ids = jnp.stack([head_ids, tail_ids], axis=-1) + 1
    slot_ids = jnp.zeros((slots, 2), jnp.int32).at[position].set(ids) - 1
    held_rows = select_rows(one_hot(slot_ids[:, 0], shard_rows), entities)
    held_tails = select_rows(one_hot(slot_ids[:, 1], shard_rows), entities)
    held_rows = held_rows.reshape(rel_count, capacity, width)

    projected = jnp.einsum(
        "rcd,rde->rce", held_rows, matrices, preferred_element_type=jnp.float32
    ).astype(jnp.bfloat16)
    slot_losses, slot_grads = score_rows(projected.reshape(slots, width), held_tails, negatives)
    grad_rows = slot_grads.reshape(rel_count, capacity, width)
    partial_value = jnp.einsum(
        "rcd,rce->rde", held_rows, grad_rows, preferred_element_type=jnp.float32
    ).astype(jnp.bfloat16)
    partial_value = partial_value.reshape(owner_count, 2, half, width, width)
    pair_sum = partial_value[:, 0].astype(jnp.float32) + swap(partial_value[:, 1], "core").astype(jnp.float32)
    pair_sum = pair_sum.astype(jnp.bfloat16).reshape(owner_count, 2, half // 2, width, width)
    group_sum = jnp.concatenate(
        [ring_reduce(pair_sum[:, 0], 1), ring_reduce(pair_sum[:, 1], -1)], axis=0
    ).astype(jnp.bfloat16)
    plane_sum = group_sum.astype(jnp.float32) + swap(group_sum, "x").astype(jnp.float32)
    other_half = swap(plane_sum, "core")
    summed = jnp.where(
        core == 0,
        jnp.concatenate([plane_sum, other_half], axis=0),
        jnp.concatenate([other_half, plane_sum], axis=0),
    )

    head_back = jnp.einsum(
        "rce,rde->rcd", grad_rows, matrices, preferred_element_type=jnp.float32
    ).astype(jnp.bfloat16)
    taken = one_hot(position, slots)
    head_grad = select_rows(taken, head_back.reshape(slots, width))
    losses = jnp.dot(taken, slot_losses, preferred_element_type=jnp.float32).astype(jnp.bfloat16)
    new_rel, new_accum = adagrad(rel_weight, rel_accum, summed)
    return (losses, head_grad, new_rel, new_accum)


GATHER_LIMIT = 16 * 1024 * 1024


def solution(mesh):
    placed = (
        P(("grp", "rel")),
        P(("grp", "rel"), None),
        P(("grp", "rel")),
        P(),
        P(("grp", "rel"), None),
        P("rel", None, None),
        P("rel", None),
    )
    outs = (
        P(("grp", "rel")),
        P(("grp", "rel"), None),
        P("rel", None, None),
        P("rel", None),
    )
    rows_step = jax.shard_map(
        per_device, mesh=mesh, in_specs=placed, out_specs=outs, check_vma=False
    )
    groups, owners = mesh.devices.shape
    split = jax.sharding.Mesh(mesh.devices.reshape(groups // 2, 2, owners), ("x", "core", "rel"))

    def respec(spec):
        return P(*[("x", "core", "rel") if part == ("grp", "rel") else part for part in spec])

    local_step = jax.shard_map(
        per_device_local,
        mesh=split,
        in_specs=tuple(respec(s) for s in placed),
        out_specs=tuple(respec(s) for s in outs),
        check_vma=False,
    )

    def step(head_ids, relations, tail_ids, neg_owner, entities, rel_weight, rel_accum):
        args = (head_ids, relations, tail_ids, neg_owner, entities, rel_weight, rel_accum)
        width = rel_weight.shape[-1]
        fits = rel_weight.shape[0] * width * width * 2 <= GATHER_LIMIT
        if owners == len(RING) and (rel_weight.shape[0] // owners) % 4 == 0 and fits:
            return local_step(*args)
        return rows_step(*args)

    return step
```

```python
import jax
import jax.numpy as jnp
from jax import lax
from jax.sharding import PartitionSpec as P

LEARNING_RATE = 1.0


def broadcast(shard, axis, root):
    mine = lax.axis_index(axis) == root
    return lax.psum(jnp.where(mine, shard, jnp.zeros_like(shard)), axis)


def score_rows(query_rows, tail_rows, negatives):
    positive = jnp.sum(query_rows.astype(jnp.float32) * tail_rows.astype(jnp.float32), axis=-1)
    neg_scores = jnp.dot(query_rows, negatives.T, preferred_element_type=jnp.float32)
    losses = jax.nn.softplus(-positive) + jnp.mean(jax.nn.softplus(neg_scores), axis=-1)
    coefs = (jax.nn.sigmoid(neg_scores) / negatives.shape[0]).astype(jnp.bfloat16)
    grad_query = -jax.nn.sigmoid(-positive)[:, None] * tail_rows.astype(jnp.float32)
    grad_query = grad_query + jnp.dot(coefs, negatives, preferred_element_type=jnp.float32)
    return (losses.astype(jnp.bfloat16), grad_query.astype(jnp.bfloat16))


def adagrad(weight, accumulator, gradient):
    new_accum = accumulator + jnp.mean(gradient * gradient, axis=-1)
    return (weight - LEARNING_RATE * gradient / jnp.sqrt(new_accum)[..., None], new_accum)


def one_hot(ids, count):
    return (ids[:, None] == jnp.arange(count, dtype=jnp.int32)[None, :]).astype(jnp.bfloat16)


def select_rows(selector, rows):
    return jnp.dot(selector, rows, preferred_element_type=jnp.float32).astype(jnp.bfloat16)


def per_device(head_ids, relations, tail_ids, neg_owner, entities, rel_weight, rel_accum):
    rows_here = head_ids.shape[0]
    width = entities.shape[1]
    shard_rows = entities.shape[0]
    owner_count = lax.axis_size("rel")
    local_rels = rel_weight.shape[0]
    rel_count = owner_count * local_rels
    capacity = 2 * rows_here // rel_count
    layout = (owner_count, local_rels, capacity)
    slots = rel_count * capacity
    negatives = broadcast(entities, ("grp", "rel"), neg_owner[0])
    rel_ids = relations[:, 0]
    rel_hot = one_hot(rel_ids, rel_count)
    order = jnp.arange(rows_here, dtype=jnp.int32)
    lower = (order[:, None] >= order[None, :]).astype(jnp.bfloat16)
    running = jnp.dot(lower, rel_hot, preferred_element_type=jnp.float32)
    rank = jnp.sum(running * rel_hot.astype(jnp.float32), axis=-1).astype(jnp.int32) - 1
    position = rel_ids * capacity + rank
    ids = jnp.stack([head_ids, tail_ids], axis=-1) + 1
    slot_ids = jnp.zeros((slots, 2), jnp.int32).at[position].set(ids) - 1
    held_rows = select_rows(one_hot(slot_ids[:, 0], shard_rows), entities).reshape(layout + (width,))
    held_rows = lax.all_to_all(held_rows, "rel", split_axis=0, concat_axis=0, tiled=True)
    tail_send = select_rows(one_hot(slot_ids[:, 1], shard_rows), entities).reshape(layout + (width,))
    held_tails = lax.all_to_all(tail_send, "rel", split_axis=0, concat_axis=0, tiled=True)
    matrices = rel_weight.astype(jnp.bfloat16)
    projected = jnp.einsum(
        "srcd,rde->srce", held_rows, matrices, preferred_element_type=jnp.float32
    ).astype(jnp.bfloat16)
    slot_losses, slot_grads = score_rows(
        projected.reshape(-1, width), held_tails.reshape(-1, width), negatives
    )
    grad_rows = slot_grads.reshape(held_rows.shape)
    partial_value = jnp.einsum(
        "srcd,srce->rde", held_rows, grad_rows, preferred_element_type=jnp.float32
    )
    summed = lax.psum(partial_value.astype(jnp.bfloat16), "grp").astype(jnp.float32)
    head_back = jnp.einsum(
        "srce,rde->srcd", grad_rows, matrices, preferred_element_type=jnp.float32
    ).astype(jnp.bfloat16)
    per_owner = local_rels * capacity
    extra = -(-per_owner // width)
    loss_rows = slot_losses.reshape(owner_count, per_owner)
    loss_rows = jnp.pad(loss_rows, ((0, 0), (0, extra * width - per_owner)))
    loss_rows = loss_rows.reshape(owner_count, extra, width)
    packed = jnp.concatenate([head_back.reshape(owner_count, per_owner, width), loss_rows], axis=1)
    packed = lax.all_to_all(packed, "rel", split_axis=0, concat_axis=0, tiled=True)
    back_grads = packed[:, :per_owner].reshape(slots, width)
    back_losses = packed[:, per_owner:].reshape(owner_count, extra * width)
    back_losses = back_losses[:, :per_owner].reshape(slots)
    taken = one_hot(position, slots)
    head_grad = select_rows(taken, back_grads)
    losses = jnp.dot(taken, back_losses, preferred_element_type=jnp.float32).astype(jnp.bfloat16)
    new_rel, new_accum = adagrad(rel_weight, rel_accum, summed)
    return (losses, head_grad, new_rel, new_accum)


RING = (0, 2, 4, 6, 7, 5, 3, 1)


def ring_tables():
    where = [0] * len(RING)
    for spot, rel in enumerate(RING):
        where[rel] = spot
    return jnp.array(RING, jnp.int32), jnp.array(where, jnp.int32)


def ring_pairs(step):
    count = len(RING)
    return [(RING[p], RING[(p + step) % count]) for p in range(count)]


def ring_collect(piece, step, ties=()):
    count = len(RING)
    order, where = ring_tables()
    me = lax.axis_index("rel")
    spot = where[me]
    out = jnp.zeros((count,) + piece.shape, piece.dtype)
    out = lax.dynamic_update_index_in_dim(out, piece, me, 0)
    current = piece
    tied = []
    for hop in range(1, count):
        if hop - 1 < len(ties) and ties[hop - 1] is not None:
            current, done = lax.optimization_barrier((current, ties[hop - 1]()))
            tied.append(done)
        current = lax.ppermute(current, "rel", ring_pairs(step))
        source = order[(spot - step * hop) % count]
        out = lax.dynamic_update_index_in_dim(out, current, source, 0)
    return out, tied


def ring_reduce(blocks, step, ties=()):
    count = len(RING)
    order, where = ring_tables()
    spot = where[lax.axis_index("rel")]

    def own(offset):
        return lax.dynamic_index_in_dim(blocks, order[(spot - step * offset) % count], 0, False)

    acc = own(1)
    tied = []
    for hop in range(1, count):
        if hop - 1 < len(ties) and ties[hop - 1] is not None:
            acc, done = lax.optimization_barrier((acc, ties[hop - 1]()))
            tied.append(done)
        received = lax.ppermute(acc, "rel", ring_pairs(step))
        total = received.astype(jnp.float32) + own(hop + 1).astype(jnp.float32)
        acc = total if hop == count - 1 else total.astype(jnp.bfloat16)
    return acc, tied


def swap(value, axis):
    return lax.ppermute(value, axis, [(0, 1), (1, 0)])


def per_device_local(head_ids, relations, tail_ids, neg_owner, entities, rel_weight, rel_accum):
    rows_here = head_ids.shape[0]
    width = entities.shape[1]
    shard_rows = entities.shape[0]
    owner_count = lax.axis_size("rel")
    local_rels = rel_weight.shape[0]
    half = local_rels // 2
    rel_count = owner_count * local_rels
    capacity = 2 * rows_here // rel_count
    slots = rel_count * capacity
    block = owner_count * capacity
    core = lax.axis_index("core")
    negatives = broadcast(entities, ("x", "core", "rel"), neg_owner[0])

    state = {}

    def tie_position():
        rel_ids = relations[:, 0]
        spot = rel_ids % local_rels
        side = (spot // half + core) % 2
        slot_rel = ((side * half + spot % half) * owner_count + rel_ids // local_rels)
        rel_hot = one_hot(slot_rel, rel_count)
        order = jnp.arange(rows_here, dtype=jnp.int32)
        lower = (order[:, None] >= order[None, :]).astype(jnp.bfloat16)
        running = jnp.dot(lower, rel_hot, preferred_element_type=jnp.float32)
        rank = jnp.sum(running * rel_hot.astype(jnp.float32), axis=-1).astype(jnp.int32) - 1
        position = slot_rel * capacity + rank
        ids = jnp.stack([head_ids, tail_ids], axis=-1) + 1
        slot_ids = jnp.zeros((slots, 2), jnp.int32).at[position].set(ids) - 1
        return (position, slot_ids)

    def tie_heads():
        return select_rows(one_hot(state["slot_ids"][:, 0], shard_rows), entities)

    def tie_tails():
        return select_rows(one_hot(state["slot_ids"][:, 1], shard_rows), entities)

    mine = lax.dynamic_slice_in_dim(rel_weight, core * half, half, 0).astype(jnp.bfloat16)
    first, tied = ring_collect(mine[0], 1, (None, tie_position))
    state["position"], state["slot_ids"] = tied[0]
    second, tied = ring_collect(mine[1], -1, (None, None, tie_heads, tie_tails))
    held_rows, held_tails = tied
    position = state["position"]
    own_blocks = [first, second]
    weights = own_blocks + [swap(first, "core"), swap(second, "core")]
    row_blocks = held_rows.reshape(len(weights), owner_count, capacity, width)

    projected = jnp.concatenate(
        [
            jnp.einsum("ocd,ode->oce", row_blocks[i], weights[i], preferred_element_type=jnp.float32)
            for i in range(len(weights))
        ],
        axis=0,
    ).astype(jnp.bfloat16)
    slot_losses, slot_grads = score_rows(projected.reshape(slots, width), held_tails, negatives)
    grad_blocks = slot_grads.reshape(len(weights), owner_count, capacity, width)

    def partial_of(i):
        return jnp.einsum(
            "ocd,oce->ode", row_blocks[i], grad_blocks[i], preferred_element_type=jnp.float32
        ).astype(jnp.bfloat16)

    pairs = [
        (partial_of(k).astype(jnp.float32) + swap(partial_of(half + k), "core").astype(jnp.float32)).astype(
            jnp.bfloat16
        )
        for k in range(half)
    ]

    def tie_back():
        return jnp.concatenate(
            [
                jnp.einsum("oce,ode->ocd", grad_blocks[i], weights[i], preferred_element_type=jnp.float32)
                for i in range(len(weights))
            ],
            axis=0,
        ).astype(jnp.bfloat16).reshape(slots, width)

    def tie_take():
        taken = one_hot(position, slots)
        head_grad = select_rows(taken, state["head_back"])
        losses = jnp.dot(taken, slot_losses, preferred_element_type=jnp.float32).astype(jnp.bfloat16)
        return (head_grad, losses)

    sum_first, tied = ring_reduce(pairs[0], 1, (None, tie_back))
    state["head_back"] = tied[0]
    sum_second, tied = ring_reduce(pairs[1], -1, (None, None, tie_take))
    head_grad, losses = tied[0]
    group_sum = jnp.stack([sum_first, sum_second], axis=0).astype(jnp.bfloat16)
    plane_sum = group_sum.astype(jnp.float32) + swap(group_sum, "x").astype(jnp.float32)
    other_half = swap(plane_sum, "core")
    summed = jnp.where(
        core == 0,
        jnp.concatenate([plane_sum, other_half], axis=0),
        jnp.concatenate([other_half, plane_sum], axis=0),
    )
    new_rel, new_accum = adagrad(rel_weight, rel_accum, summed)
    return (losses, head_grad, new_rel, new_accum)


GATHER_LIMIT = 16 * 1024 * 1024


def solution(mesh):
    placed = (
        P(("grp", "rel")),
        P(("grp", "rel"), None),
        P(("grp", "rel")),
        P(),
        P(("grp", "rel"), None),
        P("rel", None, None),
        P("rel", None),
    )
    outs = (
        P(("grp", "rel")),
        P(("grp", "rel"), None),
        P("rel", None, None),
        P("rel", None),
    )
    rows_step = jax.shard_map(
        per_device, mesh=mesh, in_specs=placed, out_specs=outs, check_vma=False
    )
    groups, owners = mesh.devices.shape
    split = jax.sharding.Mesh(mesh.devices.reshape(groups // 2, 2, owners), ("x", "core", "rel"))

    def respec(spec):
        return P(*[("x", "core", "rel") if part == ("grp", "rel") else part for part in spec])

    local_step = jax.shard_map(
        per_device_local,
        mesh=split,
        in_specs=tuple(respec(s) for s in placed),
        out_specs=tuple(respec(s) for s in outs),
        check_vma=False,
    )

    def step(head_ids, relations, tail_ids, neg_owner, entities, rel_weight, rel_accum):
        args = (head_ids, relations, tail_ids, neg_owner, entities, rel_weight, rel_accum)
        width = rel_weight.shape[-1]
        fits = rel_weight.shape[0] * width * width * 2 <= GATHER_LIMIT
        if owners == len(RING) and (rel_weight.shape[0] // owners) == 4 and fits:
            return local_step(*args)
        return rows_step(*args)

    return step
```

```python
import jax
import jax.numpy as jnp
from jax import lax
from jax.sharding import PartitionSpec as P

LEARNING_RATE = 1.0


def broadcast(shard, axis, root):
    mine = lax.axis_index(axis) == root
    return lax.psum(jnp.where(mine, shard, jnp.zeros_like(shard)), axis)


def score_rows(query_rows, tail_rows, negatives):
    positive = jnp.sum(query_rows.astype(jnp.float32) * tail_rows.astype(jnp.float32), axis=-1)
    neg_scores = jnp.dot(query_rows, negatives.T, preferred_element_type=jnp.float32)
    losses = jax.nn.softplus(-positive) + jnp.mean(jax.nn.softplus(neg_scores), axis=-1)
    coefs = (jax.nn.sigmoid(neg_scores) / negatives.shape[0]).astype(jnp.bfloat16)
    grad_query = -jax.nn.sigmoid(-positive)[:, None] * tail_rows.astype(jnp.float32)
    grad_query = grad_query + jnp.dot(coefs, negatives, preferred_element_type=jnp.float32)
    return (losses.astype(jnp.bfloat16), grad_query.astype(jnp.bfloat16))


def adagrad(weight, accumulator, gradient):
    new_accum = accumulator + jnp.mean(gradient * gradient, axis=-1)
    return (weight - LEARNING_RATE * gradient / jnp.sqrt(new_accum)[..., None], new_accum)


def one_hot(ids, count):
    return (ids[:, None] == jnp.arange(count, dtype=jnp.int32)[None, :]).astype(jnp.bfloat16)


def select_rows(selector, rows):
    return jnp.dot(selector, rows, preferred_element_type=jnp.float32).astype(jnp.bfloat16)


def per_device(head_ids, relations, tail_ids, neg_owner, entities, rel_weight, rel_accum):
    rows_here = head_ids.shape[0]
    width = entities.shape[1]
    shard_rows = entities.shape[0]
    owner_count = lax.axis_size("rel")
    local_rels = rel_weight.shape[0]
    rel_count = owner_count * local_rels
    capacity = 2 * rows_here // rel_count
    layout = (owner_count, local_rels, capacity)
    slots = rel_count * capacity
    negatives = broadcast(entities, ("grp", "rel"), neg_owner[0])
    rel_ids = relations[:, 0]
    rel_hot = one_hot(rel_ids, rel_count)
    order = jnp.arange(rows_here, dtype=jnp.int32)
    lower = (order[:, None] >= order[None, :]).astype(jnp.bfloat16)
    running = jnp.dot(lower, rel_hot, preferred_element_type=jnp.float32)
    rank = jnp.sum(running * rel_hot.astype(jnp.float32), axis=-1).astype(jnp.int32) - 1
    position = rel_ids * capacity + rank
    ids = jnp.stack([head_ids, tail_ids], axis=-1) + 1
    slot_ids = jnp.zeros((slots, 2), jnp.int32).at[position].set(ids) - 1
    held_rows = select_rows(one_hot(slot_ids[:, 0], shard_rows), entities).reshape(layout + (width,))
    held_rows = lax.all_to_all(held_rows, "rel", split_axis=0, concat_axis=0, tiled=True)
    tail_send = select_rows(one_hot(slot_ids[:, 1], shard_rows), entities).reshape(layout + (width,))
    held_tails = lax.all_to_all(tail_send, "rel", split_axis=0, concat_axis=0, tiled=True)
    matrices = rel_weight.astype(jnp.bfloat16)
    projected = jnp.einsum(
        "srcd,rde->srce", held_rows, matrices, preferred_element_type=jnp.float32
    ).astype(jnp.bfloat16)
    slot_losses, slot_grads = score_rows(
        projected.reshape(-1, width), held_tails.reshape(-1, width), negatives
    )
    grad_rows = slot_grads.reshape(held_rows.shape)
    partial_value = jnp.einsum(
        "srcd,srce->rde", held_rows, grad_rows, preferred_element_type=jnp.float32
    )
    summed = lax.psum(partial_value.astype(jnp.bfloat16), "grp").astype(jnp.float32)
    head_back = jnp.einsum(
        "srce,rde->srcd", grad_rows, matrices, preferred_element_type=jnp.float32
    ).astype(jnp.bfloat16)
    per_owner = local_rels * capacity
    extra = -(-per_owner // width)
    loss_rows = slot_losses.reshape(owner_count, per_owner)
    loss_rows = jnp.pad(loss_rows, ((0, 0), (0, extra * width - per_owner)))
    loss_rows = loss_rows.reshape(owner_count, extra, width)
    packed = jnp.concatenate([head_back.reshape(owner_count, per_owner, width), loss_rows], axis=1)
    packed = lax.all_to_all(packed, "rel", split_axis=0, concat_axis=0, tiled=True)
    back_grads = packed[:, :per_owner].reshape(slots, width)
    back_losses = packed[:, per_owner:].reshape(owner_count, extra * width)
    back_losses = back_losses[:, :per_owner].reshape(slots)
    taken = one_hot(position, slots)
    head_grad = select_rows(taken, back_grads)
    losses = jnp.dot(taken, back_losses, preferred_element_type=jnp.float32).astype(jnp.bfloat16)
    new_rel, new_accum = adagrad(rel_weight, rel_accum, summed)
    return (losses, head_grad, new_rel, new_accum)


RING = (0, 2, 4, 6, 7, 5, 3, 1)


def ring_tables():
    where = [0] * len(RING)
    for spot, rel in enumerate(RING):
        where[rel] = spot
    return jnp.array(RING, jnp.int32), jnp.array(where, jnp.int32)


def ring_pairs(step):
    count = len(RING)
    return [(RING[p], RING[(p + step) % count]) for p in range(count)]


def ring_collect(piece, step, ties=()):
    count = len(RING)
    order, where = ring_tables()
    me = lax.axis_index("rel")
    spot = where[me]
    out = jnp.zeros((count,) + piece.shape, piece.dtype)
    out = lax.dynamic_update_index_in_dim(out, piece, me, 0)
    current = piece
    tied = []
    for hop in range(1, count):
        if hop - 1 < len(ties) and ties[hop - 1] is not None:
            current, done = lax.optimization_barrier((current, ties[hop - 1]()))
            tied.append(done)
        current = lax.ppermute(current, "rel", ring_pairs(step))
        source = order[(spot - step * hop) % count]
        out = lax.dynamic_update_index_in_dim(out, current, source, 0)
    return out, tied


def ring_reduce(blocks, step, ties=()):
    count = len(RING)
    order, where = ring_tables()
    spot = where[lax.axis_index("rel")]

    def own(offset):
        return lax.dynamic_index_in_dim(blocks, order[(spot - step * offset) % count], 0, False)

    acc = own(1)
    tied = []
    for hop in range(1, count):
        if hop - 1 < len(ties) and ties[hop - 1] is not None:
            acc, done = lax.optimization_barrier((acc, ties[hop - 1]()))
            tied.append(done)
        received = lax.ppermute(acc, "rel", ring_pairs(step))
        total = received.astype(jnp.float32) + own(hop + 1).astype(jnp.float32)
        acc = total if hop == count - 1 else total.astype(jnp.bfloat16)
    return acc, tied


def swap(value, axis):
    return lax.ppermute(value, axis, [(0, 1), (1, 0)])


def per_device_local(head_ids, relations, tail_ids, neg_owner, entities, rel_weight, rel_accum):
    rows_here = head_ids.shape[0]
    width = entities.shape[1]
    shard_rows = entities.shape[0]
    owner_count = lax.axis_size("rel")
    local_rels = rel_weight.shape[0]
    half = local_rels // 2
    rel_count = owner_count * local_rels
    capacity = 2 * rows_here // rel_count
    slots = rel_count * capacity
    block = owner_count * capacity
    core = lax.axis_index("core")
    negatives = broadcast(entities, ("x", "core", "rel"), neg_owner[0])

    state = {}

    def tie_position():
        rel_ids = relations[:, 0]
        spot = rel_ids % local_rels
        side = (spot // half + core) % 2
        slot_rel = ((side * half + spot % half) * owner_count + rel_ids // local_rels)
        rel_hot = one_hot(slot_rel, rel_count)
        order = jnp.arange(rows_here, dtype=jnp.int32)
        lower = (order[:, None] >= order[None, :]).astype(jnp.bfloat16)
        running = jnp.dot(lower, rel_hot, preferred_element_type=jnp.float32)
        rank = jnp.sum(running * rel_hot.astype(jnp.float32), axis=-1).astype(jnp.int32) - 1
        position = slot_rel * capacity + rank
        ids = jnp.stack([head_ids, tail_ids], axis=-1) + 1
        slot_ids = jnp.zeros((slots, 2), jnp.int32).at[position].set(ids) - 1
        return (position, slot_ids)

    def tie_heads():
        return select_rows(one_hot(state["slot_ids"][:, 0], shard_rows), entities)

    def tie_tails():
        return select_rows(one_hot(state["slot_ids"][:, 1], shard_rows), entities)

    mine = lax.dynamic_slice_in_dim(rel_weight, core * half, half, 0).astype(jnp.bfloat16)
    first, tied = ring_collect(mine[0], 1, (None, tie_position))
    state["position"], state["slot_ids"] = tied[0]
    second, tied = ring_collect(mine[1], -1, (None, None, tie_heads, tie_tails))
    held_rows, held_tails = tied
    position = state["position"]
    own_blocks = [first, second]
    weights = own_blocks + [swap(first, "core"), swap(second, "core")]
    row_blocks = held_rows.reshape(len(weights), owner_count, capacity, width)

    projected = jnp.concatenate(
        [
            jnp.einsum("ocd,ode->oce", row_blocks[i], weights[i], preferred_element_type=jnp.float32)
            for i in range(len(weights))
        ],
        axis=0,
    ).astype(jnp.bfloat16)
    slot_losses, slot_grads = score_rows(projected.reshape(slots, width), held_tails, negatives)
    grad_blocks = slot_grads.reshape(len(weights), owner_count, capacity, width)

    def partial_of(i):
        return jnp.einsum(
            "ocd,oce->ode", row_blocks[i], grad_blocks[i], preferred_element_type=jnp.float32
        ).astype(jnp.bfloat16)

    pairs = [
        (partial_of(k).astype(jnp.float32) + swap(partial_of(half + k), "core").astype(jnp.float32)).astype(
            jnp.bfloat16
        )
        for k in range(half)
    ]

    def tie_back():
        return jnp.concatenate(
            [
                jnp.einsum("oce,ode->ocd", grad_blocks[i], weights[i], preferred_element_type=jnp.float32)
                for i in range(len(weights))
            ],
            axis=0,
        ).astype(jnp.bfloat16).reshape(slots, width)

    def tie_take():
        taken = one_hot(position, slots)
        head_grad = select_rows(taken, state["head_back"])
        losses = jnp.dot(taken, slot_losses, preferred_element_type=jnp.float32).astype(jnp.bfloat16)
        return (head_grad, losses)

    sum_first, tied = ring_reduce(pairs[0], 1, (None, tie_back))
    state["head_back"] = tied[0]
    sum_second, tied = ring_reduce(pairs[1], -1, (None, None, tie_take))
    head_grad, losses = tied[0]
    weight_half = lax.dynamic_slice_in_dim(rel_weight, core * half, half, 0)
    accum_half = lax.dynamic_slice_in_dim(rel_accum, core * half, half, 0)
    updated, accums = [], []
    for k, part in enumerate((sum_first, sum_second)):
        part = part.astype(jnp.bfloat16)
        plane = part.astype(jnp.float32) + swap(part, "x").astype(jnp.float32)
        rel_k, accum_k = adagrad(weight_half[k], accum_half[k], plane)
        updated.append(rel_k)
        accums.append(accum_k)
    mine_rel = jnp.stack(updated, axis=0)
    mine_accum = jnp.stack(accums, axis=0)
    other_rel = swap(mine_rel, "core")
    other_accum = swap(mine_accum, "core")
    first_core = core == 0
    new_rel = jnp.where(
        first_core,
        jnp.concatenate([mine_rel, other_rel], axis=0),
        jnp.concatenate([other_rel, mine_rel], axis=0),
    )
    new_accum = jnp.where(
        first_core,
        jnp.concatenate([mine_accum, other_accum], axis=0),
        jnp.concatenate([other_accum, mine_accum], axis=0),
    )
    return (losses, head_grad, new_rel, new_accum)


GATHER_LIMIT = 16 * 1024 * 1024


def solution(mesh):
    placed = (
        P(("grp", "rel")),
        P(("grp", "rel"), None),
        P(("grp", "rel")),
        P(),
        P(("grp", "rel"), None),
        P("rel", None, None),
        P("rel", None),
    )
    outs = (
        P(("grp", "rel")),
        P(("grp", "rel"), None),
        P("rel", None, None),
        P("rel", None),
    )
    rows_step = jax.shard_map(
        per_device, mesh=mesh, in_specs=placed, out_specs=outs, check_vma=False
    )
    groups, owners = mesh.devices.shape
    split = jax.sharding.Mesh(mesh.devices.reshape(groups // 2, 2, owners), ("x", "core", "rel"))

    def respec(spec):
        return P(*[("x", "core", "rel") if part == ("grp", "rel") else part for part in spec])

    local_step = jax.shard_map(
        per_device_local,
        mesh=split,
        in_specs=tuple(respec(s) for s in placed),
        out_specs=tuple(respec(s) for s in outs),
        check_vma=False,
    )

    def step(head_ids, relations, tail_ids, neg_owner, entities, rel_weight, rel_accum):
        args = (head_ids, relations, tail_ids, neg_owner, entities, rel_weight, rel_accum)
        width = rel_weight.shape[-1]
        fits = rel_weight.shape[0] * width * width * 2 <= GATHER_LIMIT
        if owners == len(RING) and (rel_weight.shape[0] // owners) == 4 and fits:
            return local_step(*args)
        return rows_step(*args)

    return step
```

```python
import jax
import jax.numpy as jnp
from jax import lax
from jax.sharding import PartitionSpec as P

LEARNING_RATE = 1.0


def broadcast(shard, axis, root):
    mine = lax.axis_index(axis) == root
    return lax.psum(jnp.where(mine, shard, jnp.zeros_like(shard)), axis)


def score_rows(query_rows, tail_rows, negatives):
    positive = jnp.sum(query_rows.astype(jnp.float32) * tail_rows.astype(jnp.float32), axis=-1)
    neg_scores = jnp.dot(query_rows, negatives.T, preferred_element_type=jnp.float32)
    losses = jax.nn.softplus(-positive) + jnp.mean(jax.nn.softplus(neg_scores), axis=-1)
    coefs = (jax.nn.sigmoid(neg_scores) / negatives.shape[0]).astype(jnp.bfloat16)
    grad_query = -jax.nn.sigmoid(-positive)[:, None] * tail_rows.astype(jnp.float32)
    grad_query = grad_query + jnp.dot(coefs, negatives, preferred_element_type=jnp.float32)
    return (losses.astype(jnp.bfloat16), grad_query.astype(jnp.bfloat16))


def adagrad(weight, accumulator, gradient):
    new_accum = accumulator + jnp.mean(gradient * gradient, axis=-1)
    return (weight - LEARNING_RATE * gradient / jnp.sqrt(new_accum)[..., None], new_accum)


def one_hot(ids, count):
    return (ids[:, None] == jnp.arange(count, dtype=jnp.int32)[None, :]).astype(jnp.bfloat16)


def select_rows(selector, rows):
    return jnp.dot(selector, rows, preferred_element_type=jnp.float32).astype(jnp.bfloat16)


def per_device(head_ids, relations, tail_ids, neg_owner, entities, rel_weight, rel_accum):
    rows_here = head_ids.shape[0]
    width = entities.shape[1]
    shard_rows = entities.shape[0]
    owner_count = lax.axis_size("rel")
    local_rels = rel_weight.shape[0]
    rel_count = owner_count * local_rels
    capacity = 2 * rows_here // rel_count
    layout = (owner_count, local_rels, capacity)
    slots = rel_count * capacity
    negatives = broadcast(entities, ("grp", "rel"), neg_owner[0])
    rel_ids = relations[:, 0]
    rel_hot = one_hot(rel_ids, rel_count)
    order = jnp.arange(rows_here, dtype=jnp.int32)
    lower = (order[:, None] >= order[None, :]).astype(jnp.bfloat16)
    running = jnp.dot(lower, rel_hot, preferred_element_type=jnp.float32)
    rank = jnp.sum(running * rel_hot.astype(jnp.float32), axis=-1).astype(jnp.int32) - 1
    position = rel_ids * capacity + rank
    ids = jnp.stack([head_ids, tail_ids], axis=-1) + 1
    slot_ids = jnp.zeros((slots, 2), jnp.int32).at[position].set(ids) - 1
    held_rows = select_rows(one_hot(slot_ids[:, 0], shard_rows), entities).reshape(layout + (width,))
    held_rows = lax.all_to_all(held_rows, "rel", split_axis=0, concat_axis=0, tiled=True)
    tail_send = select_rows(one_hot(slot_ids[:, 1], shard_rows), entities).reshape(layout + (width,))
    held_tails = lax.all_to_all(tail_send, "rel", split_axis=0, concat_axis=0, tiled=True)
    matrices = rel_weight.astype(jnp.bfloat16)
    projected = jnp.einsum(
        "srcd,rde->srce", held_rows, matrices, preferred_element_type=jnp.float32
    ).astype(jnp.bfloat16)
    slot_losses, slot_grads = score_rows(
        projected.reshape(-1, width), held_tails.reshape(-1, width), negatives
    )
    grad_rows = slot_grads.reshape(held_rows.shape)
    partial_value = jnp.einsum(
        "srcd,srce->rde", held_rows, grad_rows, preferred_element_type=jnp.float32
    )
    summed = lax.psum(partial_value.astype(jnp.bfloat16), "grp").astype(jnp.float32)
    head_back = jnp.einsum(
        "srce,rde->srcd", grad_rows, matrices, preferred_element_type=jnp.float32
    ).astype(jnp.bfloat16)
    per_owner = local_rels * capacity
    extra = -(-per_owner // width)
    loss_rows = slot_losses.reshape(owner_count, per_owner)
    loss_rows = jnp.pad(loss_rows, ((0, 0), (0, extra * width - per_owner)))
    loss_rows = loss_rows.reshape(owner_count, extra, width)
    packed = jnp.concatenate([head_back.reshape(owner_count, per_owner, width), loss_rows], axis=1)
    packed = lax.all_to_all(packed, "rel", split_axis=0, concat_axis=0, tiled=True)
    back_grads = packed[:, :per_owner].reshape(slots, width)
    back_losses = packed[:, per_owner:].reshape(owner_count, extra * width)
    back_losses = back_losses[:, :per_owner].reshape(slots)
    taken = one_hot(position, slots)
    head_grad = select_rows(taken, back_grads)
    losses = jnp.dot(taken, back_losses, preferred_element_type=jnp.float32).astype(jnp.bfloat16)
    new_rel, new_accum = adagrad(rel_weight, rel_accum, summed)
    return (losses, head_grad, new_rel, new_accum)


RING = (0, 2, 4, 6, 7, 5, 3, 1)


def ring_tables():
    where = [0] * len(RING)
    for spot, rel in enumerate(RING):
        where[rel] = spot
    return jnp.array(RING, jnp.int32), jnp.array(where, jnp.int32)


def ring_pairs(step):
    count = len(RING)
    return [(RING[p], RING[(p + step) % count]) for p in range(count)]


def ring_collect(piece, step, ties=()):
    count = len(RING)
    order, where = ring_tables()
    me = lax.axis_index("rel")
    spot = where[me]
    out = jnp.zeros((count,) + piece.shape, piece.dtype)
    out = lax.dynamic_update_index_in_dim(out, piece, me, 0)
    current = piece
    tied = []
    for hop in range(1, count):
        if hop - 1 < len(ties) and ties[hop - 1] is not None:
            current, done = lax.optimization_barrier((current, ties[hop - 1]()))
            tied.append(done)
        current = lax.ppermute(current, "rel", ring_pairs(step))
        source = order[(spot - step * hop) % count]
        out = lax.dynamic_update_index_in_dim(out, current, source, 0)
    return out, tied


def ring_collect_both(piece, ties=()):
    count = len(RING)
    order, where = ring_tables()
    me = lax.axis_index("rel")
    spot = where[me]
    out = jnp.zeros((piece.shape[0], count) + piece.shape[1:], piece.dtype)

    def put(buffer, value, index):
        return lax.dynamic_update_slice_in_dim(buffer, value[:, None], index, 1)

    out = put(out, piece, me)
    ahead, behind = piece, piece
    tied = []
    for hop in range(1, count // 2 + 1):
        if hop - 1 < len(ties) and ties[hop - 1] is not None:
            ahead, done = lax.optimization_barrier((ahead, ties[hop - 1]()))
            tied.append(done)
        ahead = lax.ppermute(ahead, "rel", ring_pairs(1))
        out = put(out, ahead, order[(spot - hop) % count])
        if hop < count - count // 2:
            behind = lax.ppermute(behind, "rel", ring_pairs(-1))
            out = put(out, behind, order[(spot + hop) % count])
    return out, tied


def ring_reduce(blocks, step, ties=()):
    count = len(RING)
    order, where = ring_tables()
    spot = where[lax.axis_index("rel")]

    def own(offset):
        return lax.dynamic_index_in_dim(blocks, order[(spot - step * offset) % count], 0, False)

    acc = own(1)
    tied = []
    for hop in range(1, count):
        if hop - 1 < len(ties) and ties[hop - 1] is not None:
            acc, done = lax.optimization_barrier((acc, ties[hop - 1]()))
            tied.append(done)
        received = lax.ppermute(acc, "rel", ring_pairs(step))
        total = received.astype(jnp.float32) + own(hop + 1).astype(jnp.float32)
        acc = total if hop == count - 1 else total.astype(jnp.bfloat16)
    return acc, tied


def swap(value, axis):
    return lax.ppermute(value, axis, [(0, 1), (1, 0)])


def per_device_local(head_ids, relations, tail_ids, neg_owner, entities, rel_weight, rel_accum):
    rows_here = head_ids.shape[0]
    width = entities.shape[1]
    shard_rows = entities.shape[0]
    owner_count = lax.axis_size("rel")
    local_rels = rel_weight.shape[0]
    half = local_rels // 2
    rel_count = owner_count * local_rels
    capacity = 2 * rows_here // rel_count
    slots = rel_count * capacity
    block = owner_count * capacity
    core = lax.axis_index("core")
    negatives = broadcast(entities, ("x", "core", "rel"), neg_owner[0])

    state = {}

    def tie_position():
        rel_ids = relations[:, 0]
        spot = rel_ids % local_rels
        side = (spot // half + core) % 2
        slot_rel = ((side * half + spot % half) * owner_count + rel_ids // local_rels)
        rel_hot = one_hot(slot_rel, rel_count)
        order = jnp.arange(rows_here, dtype=jnp.int32)
        lower = (order[:, None] >= order[None, :]).astype(jnp.bfloat16)
        running = jnp.dot(lower, rel_hot, preferred_element_type=jnp.float32)
        rank = jnp.sum(running * rel_hot.astype(jnp.float32), axis=-1).astype(jnp.int32) - 1
        position = slot_rel * capacity + rank
        ids = jnp.stack([head_ids, tail_ids], axis=-1) + 1
        slot_ids = jnp.zeros((slots, 2), jnp.int32).at[position].set(ids) - 1
        state["slot_ids"] = slot_ids
        return (position, slot_ids)

    def tie_heads():
        return select_rows(one_hot(state["slot_ids"][:, 0], shard_rows), entities)

    def tie_tails():
        return select_rows(one_hot(state["slot_ids"][:, 1], shard_rows), entities)

    mine = lax.dynamic_slice_in_dim(rel_weight, core * half, half, 0).astype(jnp.bfloat16)
    both, tied = ring_collect_both(mine, (None, tie_position, tie_heads, tie_tails))
    state["position"], state["slot_ids"] = tied[0]
    held_rows, held_tails = tied[1], tied[2]
    first, second = both[0], both[1]
    position = state["position"]
    own_blocks = [first, second]
    weights = own_blocks + [swap(first, "core"), swap(second, "core")]
    row_blocks = held_rows.reshape(len(weights), owner_count, capacity, width)

    projected = jnp.concatenate(
        [
            jnp.einsum("ocd,ode->oce", row_blocks[i], weights[i], preferred_element_type=jnp.float32)
            for i in range(len(weights))
        ],
        axis=0,
    ).astype(jnp.bfloat16)
    slot_losses, slot_grads = score_rows(projected.reshape(slots, width), held_tails, negatives)
    grad_blocks = slot_grads.reshape(len(weights), owner_count, capacity, width)

    def partial_of(i):
        return jnp.einsum(
            "ocd,oce->ode", row_blocks[i], grad_blocks[i], preferred_element_type=jnp.float32
        ).astype(jnp.bfloat16)

    pairs = [
        (partial_of(k).astype(jnp.float32) + swap(partial_of(half + k), "core").astype(jnp.float32)).astype(
            jnp.bfloat16
        )
        for k in range(half)
    ]

    def tie_back():
        return jnp.concatenate(
            [
                jnp.einsum("oce,ode->ocd", grad_blocks[i], weights[i], preferred_element_type=jnp.float32)
                for i in range(len(weights))
            ],
            axis=0,
        ).astype(jnp.bfloat16).reshape(slots, width)

    def tie_take():
        taken = one_hot(position, slots)
        head_grad = select_rows(taken, state["head_back"])
        losses = jnp.dot(taken, slot_losses, preferred_element_type=jnp.float32).astype(jnp.bfloat16)
        return (head_grad, losses)

    sum_first, tied = ring_reduce(pairs[0], 1, (None, tie_back))
    state["head_back"] = tied[0]
    sum_second, tied = ring_reduce(pairs[1], -1, (None, None, tie_take))
    head_grad, losses = tied[0]
    weight_half = lax.dynamic_slice_in_dim(rel_weight, core * half, half, 0)
    accum_half = lax.dynamic_slice_in_dim(rel_accum, core * half, half, 0)
    updated, accums = [], []
    for k, part in enumerate((sum_first, sum_second)):
        part = part.astype(jnp.bfloat16)
        plane = part.astype(jnp.float32) + swap(part, "x").astype(jnp.float32)
        rel_k, accum_k = adagrad(weight_half[k], accum_half[k], plane)
        updated.append(rel_k)
        accums.append(accum_k)
    mine_rel = jnp.stack(updated, axis=0)
    mine_accum = jnp.stack(accums, axis=0)
    other_rel = swap(mine_rel, "core")
    other_accum = swap(mine_accum, "core")
    first_core = core == 0
    new_rel = jnp.where(
        first_core,
        jnp.concatenate([mine_rel, other_rel], axis=0),
        jnp.concatenate([other_rel, mine_rel], axis=0),
    )
    new_accum = jnp.where(
        first_core,
        jnp.concatenate([mine_accum, other_accum], axis=0),
        jnp.concatenate([other_accum, mine_accum], axis=0),
    )
    return (losses, head_grad, new_rel, new_accum)


GATHER_LIMIT = 16 * 1024 * 1024


def solution(mesh):
    placed = (
        P(("grp", "rel")),
        P(("grp", "rel"), None),
        P(("grp", "rel")),
        P(),
        P(("grp", "rel"), None),
        P("rel", None, None),
        P("rel", None),
    )
    outs = (
        P(("grp", "rel")),
        P(("grp", "rel"), None),
        P("rel", None, None),
        P("rel", None),
    )
    rows_step = jax.shard_map(
        per_device, mesh=mesh, in_specs=placed, out_specs=outs, check_vma=False
    )
    groups, owners = mesh.devices.shape
    split = jax.sharding.Mesh(mesh.devices.reshape(groups // 2, 2, owners), ("x", "core", "rel"))

    def respec(spec):
        return P(*[("x", "core", "rel") if part == ("grp", "rel") else part for part in spec])

    local_step = jax.shard_map(
        per_device_local,
        mesh=split,
        in_specs=tuple(respec(s) for s in placed),
        out_specs=tuple(respec(s) for s in outs),
        check_vma=False,
    )

    def step(head_ids, relations, tail_ids, neg_owner, entities, rel_weight, rel_accum):
        args = (head_ids, relations, tail_ids, neg_owner, entities, rel_weight, rel_accum)
        width = rel_weight.shape[-1]
        fits = rel_weight.shape[0] * width * width * 2 <= GATHER_LIMIT
        if owners == len(RING) and (rel_weight.shape[0] // owners) == 4 and fits:
            return local_step(*args)
        return rows_step(*args)

    return step
```

```python
import jax
import jax.numpy as jnp
from jax import lax
from jax.sharding import PartitionSpec as P

LEARNING_RATE = 1.0


def broadcast(shard, axis, root):
    mine = lax.axis_index(axis) == root
    return lax.psum(jnp.where(mine, shard, jnp.zeros_like(shard)), axis)


def score_rows(query_rows, tail_rows, negatives):
    positive = jnp.sum(query_rows.astype(jnp.float32) * tail_rows.astype(jnp.float32), axis=-1)
    neg_scores = jnp.dot(query_rows, negatives.T, preferred_element_type=jnp.float32)
    losses = jax.nn.softplus(-positive) + jnp.mean(jax.nn.softplus(neg_scores), axis=-1)
    coefs = (jax.nn.sigmoid(neg_scores) / negatives.shape[0]).astype(jnp.bfloat16)
    grad_query = -jax.nn.sigmoid(-positive)[:, None] * tail_rows.astype(jnp.float32)
    grad_query = grad_query + jnp.dot(coefs, negatives, preferred_element_type=jnp.float32)
    return (losses.astype(jnp.bfloat16), grad_query.astype(jnp.bfloat16))


def adagrad(weight, accumulator, gradient):
    new_accum = accumulator + jnp.mean(gradient * gradient, axis=-1)
    return (weight - LEARNING_RATE * gradient / jnp.sqrt(new_accum)[..., None], new_accum)


def one_hot(ids, count):
    return (ids[:, None] == jnp.arange(count, dtype=jnp.int32)[None, :]).astype(jnp.bfloat16)


def select_rows(selector, rows):
    return jnp.dot(selector, rows, preferred_element_type=jnp.float32).astype(jnp.bfloat16)


def per_device(head_ids, relations, tail_ids, neg_owner, entities, rel_weight, rel_accum):
    rows_here = head_ids.shape[0]
    width = entities.shape[1]
    shard_rows = entities.shape[0]
    owner_count = lax.axis_size("rel")
    local_rels = rel_weight.shape[0]
    rel_count = owner_count * local_rels
    capacity = 2 * rows_here // rel_count
    layout = (owner_count, local_rels, capacity)
    slots = rel_count * capacity
    negatives = broadcast(entities, ("grp", "rel"), neg_owner[0])
    rel_ids = relations[:, 0]
    rel_hot = one_hot(rel_ids, rel_count)
    order = jnp.arange(rows_here, dtype=jnp.int32)
    lower = (order[:, None] >= order[None, :]).astype(jnp.bfloat16)
    running = jnp.dot(lower, rel_hot, preferred_element_type=jnp.float32)
    rank = jnp.sum(running * rel_hot.astype(jnp.float32), axis=-1).astype(jnp.int32) - 1
    position = rel_ids * capacity + rank
    ids = jnp.stack([head_ids, tail_ids], axis=-1) + 1
    slot_ids = jnp.zeros((slots, 2), jnp.int32).at[position].set(ids) - 1
    held_rows = select_rows(one_hot(slot_ids[:, 0], shard_rows), entities).reshape(layout + (width,))
    held_rows = lax.all_to_all(held_rows, "rel", split_axis=0, concat_axis=0, tiled=True)
    tail_send = select_rows(one_hot(slot_ids[:, 1], shard_rows), entities).reshape(layout + (width,))
    held_tails = lax.all_to_all(tail_send, "rel", split_axis=0, concat_axis=0, tiled=True)
    matrices = rel_weight.astype(jnp.bfloat16)
    projected = jnp.einsum(
        "srcd,rde->srce", held_rows, matrices, preferred_element_type=jnp.float32
    ).astype(jnp.bfloat16)
    slot_losses, slot_grads = score_rows(
        projected.reshape(-1, width), held_tails.reshape(-1, width), negatives
    )
    grad_rows = slot_grads.reshape(held_rows.shape)
    partial_value = jnp.einsum(
        "srcd,srce->rde", held_rows, grad_rows, preferred_element_type=jnp.float32
    )
    summed = lax.psum(partial_value.astype(jnp.bfloat16), "grp").astype(jnp.float32)
    head_back = jnp.einsum(
        "srce,rde->srcd", grad_rows, matrices, preferred_element_type=jnp.float32
    ).astype(jnp.bfloat16)
    per_owner = local_rels * capacity
    extra = -(-per_owner // width)
    loss_rows = slot_losses.reshape(owner_count, per_owner)
    loss_rows = jnp.pad(loss_rows, ((0, 0), (0, extra * width - per_owner)))
    loss_rows = loss_rows.reshape(owner_count, extra, width)
    packed = jnp.concatenate([head_back.reshape(owner_count, per_owner, width), loss_rows], axis=1)
    packed = lax.all_to_all(packed, "rel", split_axis=0, concat_axis=0, tiled=True)
    back_grads = packed[:, :per_owner].reshape(slots, width)
    back_losses = packed[:, per_owner:].reshape(owner_count, extra * width)
    back_losses = back_losses[:, :per_owner].reshape(slots)
    taken = one_hot(position, slots)
    head_grad = select_rows(taken, back_grads)
    losses = jnp.dot(taken, back_losses, preferred_element_type=jnp.float32).astype(jnp.bfloat16)
    new_rel, new_accum = adagrad(rel_weight, rel_accum, summed)
    return (losses, head_grad, new_rel, new_accum)


RING = (0, 2, 4, 6, 7, 5, 3, 1)


def ring_tables():
    where = [0] * len(RING)
    for spot, rel in enumerate(RING):
        where[rel] = spot
    return jnp.array(RING, jnp.int32), jnp.array(where, jnp.int32)


def ring_pairs(step):
    count = len(RING)
    return [(RING[p], RING[(p + step) % count]) for p in range(count)]


def ring_collect(piece, step, ties=()):
    count = len(RING)
    order, where = ring_tables()
    me = lax.axis_index("rel")
    spot = where[me]
    out = jnp.zeros((count,) + piece.shape, piece.dtype)
    out = lax.dynamic_update_index_in_dim(out, piece, me, 0)
    current = piece
    tied = []
    for hop in range(1, count):
        if hop - 1 < len(ties) and ties[hop - 1] is not None:
            current, done = lax.optimization_barrier((current, ties[hop - 1]()))
            tied.append(done)
        current = lax.ppermute(current, "rel", ring_pairs(step))
        source = order[(spot - step * hop) % count]
        out = lax.dynamic_update_index_in_dim(out, current, source, 0)
    return out, tied


def ring_collect_both(piece, ties=(), back_ties=()):
    count = len(RING)
    order, where = ring_tables()
    me = lax.axis_index("rel")
    spot = where[me]
    out = jnp.zeros((piece.shape[0], count) + piece.shape[1:], piece.dtype)

    def put(buffer, value, index):
        return lax.dynamic_update_slice_in_dim(buffer, value[:, None], index, 1)

    out = put(out, piece, me)
    ahead, behind = piece, piece
    tied = []
    for hop in range(1, count // 2 + 1):
        if hop - 1 < len(ties) and ties[hop - 1] is not None:
            ahead, done = lax.optimization_barrier((ahead, ties[hop - 1]()))
            tied.append(done)
        ahead = lax.ppermute(ahead, "rel", ring_pairs(1))
        out = put(out, ahead, order[(spot - hop) % count])
        if hop < count - count // 2:
            if hop - 1 < len(back_ties) and back_ties[hop - 1] is not None:
                behind, done = lax.optimization_barrier((behind, back_ties[hop - 1]()))
                tied.append(done)
            behind = lax.ppermute(behind, "rel", ring_pairs(-1))
            out = put(out, behind, order[(spot + hop) % count])
    return out, tied


def ring_reduce(blocks, step, ties=()):
    count = len(RING)
    order, where = ring_tables()
    spot = where[lax.axis_index("rel")]

    def own(offset):
        return lax.dynamic_index_in_dim(blocks, order[(spot - step * offset) % count], 0, False)

    acc = own(1)
    tied = []
    for hop in range(1, count):
        if hop - 1 < len(ties) and ties[hop - 1] is not None:
            acc, done = lax.optimization_barrier((acc, ties[hop - 1]()))
            tied.append(done)
        received = lax.ppermute(acc, "rel", ring_pairs(step))
        total = received.astype(jnp.float32) + own(hop + 1).astype(jnp.float32)
        acc = total if hop == count - 1 else total.astype(jnp.bfloat16)
    return acc, tied


def swap(value, axis):
    return lax.ppermute(value, axis, [(0, 1), (1, 0)])


def per_device_local(head_ids, relations, tail_ids, neg_owner, entities, rel_weight, rel_accum):
    rows_here = head_ids.shape[0]
    width = entities.shape[1]
    shard_rows = entities.shape[0]
    owner_count = lax.axis_size("rel")
    local_rels = rel_weight.shape[0]
    half = local_rels // 2
    rel_count = owner_count * local_rels
    capacity = 2 * rows_here // rel_count
    slots = rel_count * capacity
    block = owner_count * capacity
    core = lax.axis_index("core")
    negatives = broadcast(entities, ("x", "core", "rel"), neg_owner[0])

    state = {}

    def tie_position():
        rel_ids = relations[:, 0]
        spot = rel_ids % local_rels
        side = (spot // half + core) % 2
        slot_rel = ((side * half + spot % half) * owner_count + rel_ids // local_rels)
        rel_hot = one_hot(slot_rel, rel_count)
        order = jnp.arange(rows_here, dtype=jnp.int32)
        lower = (order[:, None] >= order[None, :]).astype(jnp.bfloat16)
        running = jnp.dot(lower, rel_hot, preferred_element_type=jnp.float32)
        rank = jnp.sum(running * rel_hot.astype(jnp.float32), axis=-1).astype(jnp.int32) - 1
        position = slot_rel * capacity + rank
        ids = jnp.stack([head_ids, tail_ids], axis=-1) + 1
        slot_ids = jnp.zeros((slots, 2), jnp.int32).at[position].set(ids) - 1
        state["slot_ids"] = slot_ids
        return (position, slot_ids)

    def tie_heads():
        return select_rows(one_hot(state["slot_ids"][:, 0], shard_rows), entities)

    def tie_tails():
        return select_rows(one_hot(state["slot_ids"][:, 1], shard_rows), entities)

    mine = lax.dynamic_slice_in_dim(rel_weight, core * half, half, 0).astype(jnp.bfloat16)
    both, tied = ring_collect_both(mine, (None, None, None, tie_tails), (None, tie_position, tie_heads))
    state["position"], state["slot_ids"] = tied[0]
    held_rows, held_tails = tied[1], tied[2]
    first, second = both[0], both[1]
    position = state["position"]
    own_blocks = [first, second]
    weights = own_blocks + [swap(first, "core"), swap(second, "core")]
    row_blocks = held_rows.reshape(len(weights), owner_count, capacity, width)

    projected = jnp.concatenate(
        [
            jnp.einsum("ocd,ode->oce", row_blocks[i], weights[i], preferred_element_type=jnp.float32)
            for i in range(len(weights))
        ],
        axis=0,
    ).astype(jnp.bfloat16)
    slot_losses, slot_grads = score_rows(projected.reshape(slots, width), held_tails, negatives)
    grad_blocks = slot_grads.reshape(len(weights), owner_count, capacity, width)

    def partial_of(i):
        return jnp.einsum(
            "ocd,oce->ode", row_blocks[i], grad_blocks[i], preferred_element_type=jnp.float32
        ).astype(jnp.bfloat16)

    pairs = [
        (partial_of(k).astype(jnp.float32) + swap(partial_of(half + k), "core").astype(jnp.float32)).astype(
            jnp.bfloat16
        )
        for k in range(half)
    ]

    def tie_back():
        return jnp.concatenate(
            [
                jnp.einsum("oce,ode->ocd", grad_blocks[i], weights[i], preferred_element_type=jnp.float32)
                for i in range(len(weights))
            ],
            axis=0,
        ).astype(jnp.bfloat16).reshape(slots, width)

    def tie_take():
        taken = one_hot(position, slots)
        head_grad = select_rows(taken, state["head_back"])
        losses = jnp.dot(taken, slot_losses, preferred_element_type=jnp.float32).astype(jnp.bfloat16)
        return (head_grad, losses)

    sum_first, tied = ring_reduce(pairs[0], 1, (None, tie_back))
    state["head_back"] = tied[0]
    sum_second, tied = ring_reduce(pairs[1], -1, (None, None, tie_take))
    head_grad, losses = tied[0]
    weight_half = lax.dynamic_slice_in_dim(rel_weight, core * half, half, 0)
    accum_half = lax.dynamic_slice_in_dim(rel_accum, core * half, half, 0)
    updated, accums = [], []
    for k, part in enumerate((sum_first, sum_second)):
        part = part.astype(jnp.bfloat16)
        plane = part.astype(jnp.float32) + swap(part, "x").astype(jnp.float32)
        rel_k, accum_k = adagrad(weight_half[k], accum_half[k], plane)
        updated.append(rel_k)
        accums.append(accum_k)
    mine_rel = jnp.stack(updated, axis=0)
    mine_accum = jnp.stack(accums, axis=0)
    other_rel = swap(mine_rel, "core")
    other_accum = swap(mine_accum, "core")
    first_core = core == 0
    new_rel = jnp.where(
        first_core,
        jnp.concatenate([mine_rel, other_rel], axis=0),
        jnp.concatenate([other_rel, mine_rel], axis=0),
    )
    new_accum = jnp.where(
        first_core,
        jnp.concatenate([mine_accum, other_accum], axis=0),
        jnp.concatenate([other_accum, mine_accum], axis=0),
    )
    return (losses, head_grad, new_rel, new_accum)


GATHER_LIMIT = 16 * 1024 * 1024


def solution(mesh):
    placed = (
        P(("grp", "rel")),
        P(("grp", "rel"), None),
        P(("grp", "rel")),
        P(),
        P(("grp", "rel"), None),
        P("rel", None, None),
        P("rel", None),
    )
    outs = (
        P(("grp", "rel")),
        P(("grp", "rel"), None),
        P("rel", None, None),
        P("rel", None),
    )
    rows_step = jax.shard_map(
        per_device, mesh=mesh, in_specs=placed, out_specs=outs, check_vma=False
    )
    groups, owners = mesh.devices.shape
    split = jax.sharding.Mesh(mesh.devices.reshape(groups // 2, 2, owners), ("x", "core", "rel"))

    def respec(spec):
        return P(*[("x", "core", "rel") if part == ("grp", "rel") else part for part in spec])

    local_step = jax.shard_map(
        per_device_local,
        mesh=split,
        in_specs=tuple(respec(s) for s in placed),
        out_specs=tuple(respec(s) for s in outs),
        check_vma=False,
    )

    def step(head_ids, relations, tail_ids, neg_owner, entities, rel_weight, rel_accum):
        args = (head_ids, relations, tail_ids, neg_owner, entities, rel_weight, rel_accum)
        width = rel_weight.shape[-1]
        fits = rel_weight.shape[0] * width * width * 2 <= GATHER_LIMIT
        if owners == len(RING) and (rel_weight.shape[0] // owners) == 4 and fits:
            return local_step(*args)
        return rows_step(*args)

    return step
```

```python
import jax
import jax.numpy as jnp
from jax import lax
from jax.sharding import PartitionSpec as P

LEARNING_RATE = 1.0


def broadcast(shard, axis, root):
    mine = lax.axis_index(axis) == root
    return lax.psum(jnp.where(mine, shard, jnp.zeros_like(shard)), axis)


def score_rows(query_rows, tail_rows, negatives):
    positive = jnp.sum(query_rows.astype(jnp.float32) * tail_rows.astype(jnp.float32), axis=-1)
    neg_scores = jnp.dot(query_rows, negatives.T, preferred_element_type=jnp.float32)
    losses = jax.nn.softplus(-positive) + jnp.mean(jax.nn.softplus(neg_scores), axis=-1)
    coefs = (jax.nn.sigmoid(neg_scores) / negatives.shape[0]).astype(jnp.bfloat16)
    grad_query = -jax.nn.sigmoid(-positive)[:, None] * tail_rows.astype(jnp.float32)
    grad_query = grad_query + jnp.dot(coefs, negatives, preferred_element_type=jnp.float32)
    return (losses.astype(jnp.bfloat16), grad_query.astype(jnp.bfloat16))


def adagrad(weight, accumulator, gradient):
    new_accum = accumulator + jnp.mean(gradient * gradient, axis=-1)
    return (weight - LEARNING_RATE * gradient / jnp.sqrt(new_accum)[..., None], new_accum)


def one_hot(ids, count):
    return (ids[:, None] == jnp.arange(count, dtype=jnp.int32)[None, :]).astype(jnp.bfloat16)


def select_rows(selector, rows):
    return jnp.dot(selector, rows, preferred_element_type=jnp.float32).astype(jnp.bfloat16)


def per_device(head_ids, relations, tail_ids, neg_owner, entities, rel_weight, rel_accum):
    rows_here = head_ids.shape[0]
    width = entities.shape[1]
    shard_rows = entities.shape[0]
    owner_count = lax.axis_size("rel")
    local_rels = rel_weight.shape[0]
    rel_count = owner_count * local_rels
    capacity = 2 * rows_here // rel_count
    layout = (owner_count, local_rels, capacity)
    slots = rel_count * capacity
    negatives = broadcast(entities, ("grp", "rel"), neg_owner[0])
    rel_ids = relations[:, 0]
    rel_hot = one_hot(rel_ids, rel_count)
    order = jnp.arange(rows_here, dtype=jnp.int32)
    lower = (order[:, None] >= order[None, :]).astype(jnp.bfloat16)
    running = jnp.dot(lower, rel_hot, preferred_element_type=jnp.float32)
    rank = jnp.sum(running * rel_hot.astype(jnp.float32), axis=-1).astype(jnp.int32) - 1
    position = rel_ids * capacity + rank
    ids = jnp.stack([head_ids, tail_ids], axis=-1) + 1
    slot_ids = jnp.zeros((slots, 2), jnp.int32).at[position].set(ids) - 1
    held_rows = select_rows(one_hot(slot_ids[:, 0], shard_rows), entities).reshape(layout + (width,))
    held_rows = lax.all_to_all(held_rows, "rel", split_axis=0, concat_axis=0, tiled=True)
    tail_send = select_rows(one_hot(slot_ids[:, 1], shard_rows), entities).reshape(layout + (width,))
    held_tails = lax.all_to_all(tail_send, "rel", split_axis=0, concat_axis=0, tiled=True)
    matrices = rel_weight.astype(jnp.bfloat16)
    projected = jnp.einsum(
        "srcd,rde->srce", held_rows, matrices, preferred_element_type=jnp.float32
    ).astype(jnp.bfloat16)
    slot_losses, slot_grads = score_rows(
        projected.reshape(-1, width), held_tails.reshape(-1, width), negatives
    )
    grad_rows = slot_grads.reshape(held_rows.shape)
    partial_value = jnp.einsum(
        "srcd,srce->rde", held_rows, grad_rows, preferred_element_type=jnp.float32
    )
    summed = lax.psum(partial_value.astype(jnp.bfloat16), "grp").astype(jnp.float32)
    head_back = jnp.einsum(
        "srce,rde->srcd", grad_rows, matrices, preferred_element_type=jnp.float32
    ).astype(jnp.bfloat16)
    per_owner = local_rels * capacity
    extra = -(-per_owner // width)
    loss_rows = slot_losses.reshape(owner_count, per_owner)
    loss_rows = jnp.pad(loss_rows, ((0, 0), (0, extra * width - per_owner)))
    loss_rows = loss_rows.reshape(owner_count, extra, width)
    packed = jnp.concatenate([head_back.reshape(owner_count, per_owner, width), loss_rows], axis=1)
    packed = lax.all_to_all(packed, "rel", split_axis=0, concat_axis=0, tiled=True)
    back_grads = packed[:, :per_owner].reshape(slots, width)
    back_losses = packed[:, per_owner:].reshape(owner_count, extra * width)
    back_losses = back_losses[:, :per_owner].reshape(slots)
    taken = one_hot(position, slots)
    head_grad = select_rows(taken, back_grads)
    losses = jnp.dot(taken, back_losses, preferred_element_type=jnp.float32).astype(jnp.bfloat16)
    new_rel, new_accum = adagrad(rel_weight, rel_accum, summed)
    return (losses, head_grad, new_rel, new_accum)


RING = (0, 2, 4, 6, 7, 5, 3, 1)


def ring_tables():
    where = [0] * len(RING)
    for spot, rel in enumerate(RING):
        where[rel] = spot
    return jnp.array(RING, jnp.int32), jnp.array(where, jnp.int32)


def ring_pairs(step):
    count = len(RING)
    return [(RING[p], RING[(p + step) % count]) for p in range(count)]


def ring_collect(piece, step, ties=()):
    count = len(RING)
    order, where = ring_tables()
    me = lax.axis_index("rel")
    spot = where[me]
    out = jnp.zeros((count,) + piece.shape, piece.dtype)
    out = lax.dynamic_update_index_in_dim(out, piece, me, 0)
    current = piece
    tied = []
    for hop in range(1, count):
        if hop - 1 < len(ties) and ties[hop - 1] is not None:
            current, done = lax.optimization_barrier((current, ties[hop - 1]()))
            tied.append(done)
        current = lax.ppermute(current, "rel", ring_pairs(step))
        source = order[(spot - step * hop) % count]
        out = lax.dynamic_update_index_in_dim(out, current, source, 0)
    return out, tied


def ring_collect_both(piece, ties=(), back_ties=()):
    count = len(RING)
    order, where = ring_tables()
    me = lax.axis_index("rel")
    spot = where[me]
    out = jnp.zeros((piece.shape[0], count) + piece.shape[1:], piece.dtype)

    def put(buffer, value, index):
        return lax.dynamic_update_slice_in_dim(buffer, value[:, None], index, 1)

    out = put(out, piece, me)
    ahead, behind = piece, piece
    tied = []
    for hop in range(1, count // 2 + 1):
        if hop - 1 < len(ties) and ties[hop - 1] is not None:
            ahead, done = lax.optimization_barrier((ahead, ties[hop - 1]()))
            tied.append(done)
        ahead = lax.ppermute(ahead, "rel", ring_pairs(1))
        out = put(out, ahead, order[(spot - hop) % count])
        if hop < count - count // 2:
            if hop - 1 < len(back_ties) and back_ties[hop - 1] is not None:
                behind, done = lax.optimization_barrier((behind, back_ties[hop - 1]()))
                tied.append(done)
            behind = lax.ppermute(behind, "rel", ring_pairs(-1))
            out = put(out, behind, order[(spot + hop) % count])
    return out, tied


def ring_reduce(blocks, step, ties=()):
    count = len(RING)
    order, where = ring_tables()
    spot = where[lax.axis_index("rel")]

    def own(offset):
        return lax.dynamic_index_in_dim(blocks, order[(spot - step * offset) % count], 0, False)

    acc = own(1)
    tied = []
    for hop in range(1, count):
        if hop - 1 < len(ties) and ties[hop - 1] is not None:
            acc, done = lax.optimization_barrier((acc, ties[hop - 1]()))
            tied.append(done)
        received = lax.ppermute(acc, "rel", ring_pairs(step))
        total = received.astype(jnp.float32) + own(hop + 1).astype(jnp.float32)
        acc = total if hop == count - 1 else total.astype(jnp.bfloat16)
    return acc, tied


def swap(value, axis):
    return lax.ppermute(value, axis, [(0, 1), (1, 0)])


def per_device_local(head_ids, relations, tail_ids, neg_owner, entities, rel_weight, rel_accum):
    rows_here = head_ids.shape[0]
    width = entities.shape[1]
    shard_rows = entities.shape[0]
    owner_count = lax.axis_size("rel")
    local_rels = rel_weight.shape[0]
    half = local_rels // 2
    rel_count = owner_count * local_rels
    capacity = 2 * rows_here // rel_count
    slots = rel_count * capacity
    block = owner_count * capacity
    core = lax.axis_index("core")
    negatives = broadcast(entities, ("x", "core", "rel"), neg_owner[0])

    state = {}

    def tie_position():
        rel_ids = relations[:, 0]
        spot = rel_ids % local_rels
        side = (spot // half + core) % 2
        slot_rel = ((side * half + spot % half) * owner_count + rel_ids // local_rels)
        rel_hot = one_hot(slot_rel, rel_count)
        order = jnp.arange(rows_here, dtype=jnp.int32)
        lower = (order[:, None] >= order[None, :]).astype(jnp.bfloat16)
        running = jnp.dot(lower, rel_hot, preferred_element_type=jnp.float32)
        rank = jnp.sum(running * rel_hot.astype(jnp.float32), axis=-1).astype(jnp.int32) - 1
        position = slot_rel * capacity + rank
        ids = jnp.stack([head_ids, tail_ids], axis=-1) + 1
        slot_ids = jnp.zeros((slots, 2), jnp.int32).at[position].set(ids) - 1
        state["slot_ids"] = slot_ids
        return (position, slot_ids)

    def tie_heads():
        return select_rows(one_hot(state["slot_ids"][:, 0], shard_rows), entities)

    def tie_tails():
        return select_rows(one_hot(state["slot_ids"][:, 1], shard_rows), entities)

    mine = lax.dynamic_slice_in_dim(rel_weight, core * half, half, 0).astype(jnp.bfloat16)
    both, tied = ring_collect_both(mine, (None, None, None, tie_tails), (None, tie_position, tie_heads))
    state["position"], state["slot_ids"] = tied[0]
    held_rows, held_tails = tied[1], tied[2]
    first, second = both[0], both[1]
    position = state["position"]
    own_blocks = [first, second]
    weights = own_blocks + [swap(first, "core"), swap(second, "core")]
    row_blocks = held_rows.reshape(len(weights), owner_count, capacity, width)

    projected = jnp.concatenate(
        [
            jnp.einsum("ocd,ode->oce", row_blocks[i], weights[i], preferred_element_type=jnp.float32)
            for i in range(len(weights))
        ],
        axis=0,
    ).astype(jnp.bfloat16)
    slot_losses, slot_grads = score_rows(projected.reshape(slots, width), held_tails, negatives)
    grad_blocks = slot_grads.reshape(len(weights), owner_count, capacity, width)

    def partial_of(i):
        return jnp.einsum(
            "ocd,oce->ode", row_blocks[i], grad_blocks[i], preferred_element_type=jnp.float32
        ).astype(jnp.bfloat16)

    pairs = [
        (partial_of(k).astype(jnp.float32) + swap(partial_of(half + k), "core").astype(jnp.float32)).astype(
            jnp.bfloat16
        )
        for k in range(half)
    ]

    def tie_back():
        return jnp.concatenate(
            [
                jnp.einsum("oce,ode->ocd", grad_blocks[i], weights[i], preferred_element_type=jnp.float32)
                for i in range(len(weights))
            ],
            axis=0,
        ).astype(jnp.bfloat16).reshape(slots, width)

    def tie_take():
        taken = one_hot(position, slots)
        head_grad = select_rows(taken, state["head_back"])
        losses = jnp.dot(taken, slot_losses, preferred_element_type=jnp.float32).astype(jnp.bfloat16)
        return (head_grad, losses)

    sum_first, tied = ring_reduce(pairs[0], 1, (None, tie_back))
    state["head_back"] = tied[0]
    sum_second, tied = ring_reduce(pairs[1], -1, (None, None, tie_take))
    head_grad, losses = tied[0]
    weight_half = lax.dynamic_slice_in_dim(rel_weight, core * half, half, 0)
    accum_half = lax.dynamic_slice_in_dim(rel_accum, core * half, half, 0)
    mine_rel, mine_accum, other_rel, other_accum = [], [], [], []
    for k, part in enumerate((sum_first, sum_second)):
        part = part.astype(jnp.bfloat16)
        plane = part.astype(jnp.float32) + swap(part, "x").astype(jnp.float32)
        rel_k, accum_k = adagrad(weight_half[k], accum_half[k], plane)
        mine_rel.append(rel_k)
        mine_accum.append(accum_k)
        other_rel.append(swap(rel_k, "core"))
        other_accum.append(swap(accum_k, "core"))
    first_core = core == 0
    new_rel = jnp.where(
        first_core,
        jnp.stack(mine_rel + other_rel, axis=0),
        jnp.stack(other_rel + mine_rel, axis=0),
    )
    new_accum = jnp.where(
        first_core,
        jnp.stack(mine_accum + other_accum, axis=0),
        jnp.stack(other_accum + mine_accum, axis=0),
    )
    return (losses, head_grad, new_rel, new_accum)


GATHER_LIMIT = 16 * 1024 * 1024


def solution(mesh):
    placed = (
        P(("grp", "rel")),
        P(("grp", "rel"), None),
        P(("grp", "rel")),
        P(),
        P(("grp", "rel"), None),
        P("rel", None, None),
        P("rel", None),
    )
    outs = (
        P(("grp", "rel")),
        P(("grp", "rel"), None),
        P("rel", None, None),
        P("rel", None),
    )
    rows_step = jax.shard_map(
        per_device, mesh=mesh, in_specs=placed, out_specs=outs, check_vma=False
    )
    groups, owners = mesh.devices.shape
    split = jax.sharding.Mesh(mesh.devices.reshape(groups // 2, 2, owners), ("x", "core", "rel"))

    def respec(spec):
        return P(*[("x", "core", "rel") if part == ("grp", "rel") else part for part in spec])

    local_step = jax.shard_map(
        per_device_local,
        mesh=split,
        in_specs=tuple(respec(s) for s in placed),
        out_specs=tuple(respec(s) for s in outs),
        check_vma=False,
    )

    def step(head_ids, relations, tail_ids, neg_owner, entities, rel_weight, rel_accum):
        args = (head_ids, relations, tail_ids, neg_owner, entities, rel_weight, rel_accum)
        width = rel_weight.shape[-1]
        fits = rel_weight.shape[0] * width * width * 2 <= GATHER_LIMIT
        if owners == len(RING) and (rel_weight.shape[0] // owners) == 4 and fits:
            return local_step(*args)
        return rows_step(*args)

    return step
```
